512 devices in a mesh: chan: 128 (over x, z_hi, y, core), seg: 4 (over z_lo).
Axes of the slice: x: 4, y: 8, z: 8 (z_hi: 2, z_lo: 4; z = z_hi * 4 + z_lo), core: 2. Of those that a mesh axis runs over, the one named last changes fastest.
Arguments:
- spectra: bfloat16 [2, 32, 4096, 512], P(None, 'seg', 'chan'), may hold values from -6 to 6
- sources: int32 [8, 4], replicated, may hold values from 0 to 4095, as said below
Outputs:
- correlations: float32 [32, 4096, 512], P(None, ('chan', 'seg'))
The draws below stay inside these ranges and needn't reach their ends.
Inputs may be any that keep to these rules, and one draw needn't show every extreme that they name: `sources`: each entry names a channel of the array; entries may repeat and may crowd onto the channels of a few devices of chan.
All inputs are finite; a program needn't handle non-finite values.
Results may differ from the reference program's by a relative error of at most 0.004.
Values may be sent and summed in bfloat16 or wider, within the bound.
No kernel may reach another device: no remote copies, remote signals or barrier semaphores. Data moves between devices by JAX's collectives and lax.ppermute only.
A program may use at most 128 MiB of HBM per device.

```python
import math
import jax
import jax.numpy as jnp
from jax import lax

FREQS = 512
LAGS = 256
CH_DEV = 32
BATCHES = 8
PER_BATCH = 4
CHANNELS = 4096
SEGMENTS = 32
SOURCES = 32


def draw_sources(key, part):
    owners_count = CHANNELS // CH_DEV
    keys = jax.random.split(jax.random.fold_in(key, 7), 5)
    hubs = jax.random.randint(keys[0], (4,), 0, owners_count)
    pick = jax.random.randint(keys[1], (BATCHES, PER_BATCH), 0, 4)
    crowded = hubs[pick]
    anywhere = jax.random.randint(keys[2], (BATCHES, PER_BATCH), 0, owners_count)
    use_hub = jax.random.randint(keys[3], (BATCHES, PER_BATCH), 0, 2) == 1
    owner = jnp.where(use_hub, crowded, anywhere)
    offset = jax.random.randint(keys[4], (BATCHES, PER_BATCH), 0, CH_DEV)
    return (owner * CH_DEV + offset).astype(jnp.int32)


def level_of(key, shape, cuts, smallest, largest):
    def one(position, parts):
        heights = jax.random.uniform(jax.random.fold_in(jax.random.fold_in(key, 6), position), (parts,), jnp.float32, smallest / len(cuts), largest / len(cuts))
        return jnp.repeat(jnp.exp(heights), shape[position] // parts).reshape((-1,) + (1,) * (len(shape) - position - 1))

    loudness = one(*cuts[0])
    for cut in cuts[1:]:
        loudness = loudness * one(*cut)
    return loudness


def scatter_about(own_key, dims, deviation, most, cuts=(), held_as=jnp.bfloat16):
    values = jax.random.normal(own_key, dims, jnp.float32) * deviation
    if len(cuts) > 0:
        values = level_of(own_key, dims, cuts, -0.22, 0.18) * values
    return jnp.clip(values, min=-most, max=most).astype(held_as)


def setup_inputs(seed: int = 0) -> dict:
    splits = jax.random.split(jax.random.key(seed), 3)
    return {
        "spectra": scatter_about(splits[0], (2, SEGMENTS, CHANNELS, FREQS), 1.0, 6.0, ((1, 4), (2, 128))),
        "sources": draw_sources(jax.random.fold_in(splits[2], 71), 0),
    }


def whiten(spectra):
    values = spectra.astype(jnp.float32)
    power_mean = lax.optimization_barrier(jnp.mean(values[0] * values[0] + values[1] * values[1], axis=-1))
    inv_scale = lax.rsqrt(power_mean + 1e-06)
    return (values * inv_scale[None, :, :, None]).astype(jnp.bfloat16)

def lag_matrix(freqs, half_lags):
    period = 2 * freqs
    rows = jnp.arange(freqs, dtype=jnp.int32)
    shifts = jnp.arange(2 * half_lags, dtype=jnp.int32) - half_lags
    phase = jnp.mod(rows[:, None] * shifts[None, :], period)
    angles = phase.astype(jnp.float32) * (2.0 * math.pi / period)
    return jnp.concatenate([jnp.cos(angles), -jnp.sin(angles)], axis=0)

def correlate_ref(source_spec, receiver_spec, lag_table):
    segs = receiver_spec.shape[1]
    freqs = receiver_spec.shape[3]
    high = lax.Precision.HIGHEST
    real_part = jnp.einsum('pkf,krf->prf', source_spec[0], receiver_spec[0], precision=high) + jnp.einsum('pkf,krf->prf', source_spec[1], receiver_spec[1], precision=high)
    imag_part = jnp.einsum('pkf,krf->prf', source_spec[0], receiver_spec[1], precision=high) - jnp.einsum('pkf,krf->prf', source_spec[1], receiver_spec[0], precision=high)
    stacked = jnp.concatenate([real_part, imag_part], axis=-1) * (1.0 / math.sqrt(segs))
    flat = stacked.reshape(-1, 2 * freqs)
    result = jnp.dot(flat, lag_table, precision=high, preferred_element_type=jnp.float32) * (1.0 / math.sqrt(freqs))
    return result.reshape(stacked.shape[0], stacked.shape[1], -1)

def reference(spectra, sources):
    blocks_count = CHANNELS // CH_DEV
    blocks = spectra.reshape(2, SEGMENTS, blocks_count, CH_DEV, FREQS).transpose(2, 0, 1, 3, 4)
    whitened = lax.map(whiten, blocks).transpose(1, 2, 0, 3, 4).reshape(2, SEGMENTS, CHANNELS, FREQS)
    lag_table = lag_matrix(FREQS, LAGS)

    def one_batch(ids):
        chosen = jnp.take(whitened, ids, axis=2)
        chosen = jnp.transpose(chosen, (0, 2, 1, 3)).astype(jnp.float32)

        def one_block(start):
            receivers = lax.dynamic_slice_in_dim(whitened, start, CH_DEV, 2).astype(jnp.float32)
            return correlate_ref(chosen, receivers, lag_table)
        starts = jnp.arange(blocks_count, dtype=jnp.int32) * CH_DEV
        pieces = lax.map(one_block, starts)
        return jnp.transpose(pieces, (1, 0, 2, 3)).reshape(PER_BATCH, CHANNELS, 2 * LAGS)
    output = lax.map(one_batch, sources)
    return output.reshape(SOURCES, CHANNELS, 2 * LAGS)
```

```python
import math

import jax
import jax.numpy as jnp
from jax import lax
from jax.sharding import Mesh, PartitionSpec as P

LAGS = 256
CHAN_FACTORS = (("x", 4), ("zh", 2), ("y", 8), ("c", 2))
CHAN_AXES = tuple(name for name, _ in CHAN_FACTORS)
REDUCE_ORDER = ("c", "y", "zh", "x")


def whiten(spectra):
    values = spectra.astype(jnp.float32)
    power_mean = jnp.mean(values[0] * values[0] + values[1] * values[1], axis=-1)
    inv_scale = lax.rsqrt(power_mean + 1e-06)
    return (values * inv_scale[None, :, :, None]).astype(jnp.bfloat16)


def lag_matrix(freqs, half_lags):
    period = 2 * freqs
    rows = jnp.arange(freqs, dtype=jnp.int32)
    shifts = jnp.arange(2 * half_lags, dtype=jnp.int32) - half_lags
    phase = jnp.mod(rows[:, None] * shifts[None, :], period)
    angles = phase.astype(jnp.float32) * (2.0 * math.pi / period)
    return jnp.concatenate([jnp.cos(angles), -jnp.sin(angles)], axis=0)


def correlate(source_spec, receiver_spec, lag_table):
    segs = receiver_spec.shape[1]
    freqs = receiver_spec.shape[3]
    real_part = jnp.einsum(
        "pkf,krf->prf", source_spec[0], receiver_spec[0], preferred_element_type=jnp.float32
    ) + jnp.einsum(
        "pkf,krf->prf", source_spec[1], receiver_spec[1], preferred_element_type=jnp.float32
    )
    imag_part = jnp.einsum(
        "pkf,krf->prf", source_spec[0], receiver_spec[1], preferred_element_type=jnp.float32
    ) - jnp.einsum(
        "pkf,krf->prf", source_spec[1], receiver_spec[0], preferred_element_type=jnp.float32
    )
    stacked = jnp.concatenate([real_part, imag_part], axis=-1) * (1.0 / math.sqrt(segs))
    flat = stacked.reshape(-1, 2 * freqs)
    result = jnp.dot(
        flat, lag_table, precision=lax.Precision.HIGHEST, preferred_element_type=jnp.float32
    ) * (1.0 / math.sqrt(freqs))
    return result.reshape(stacked.shape[0], stacked.shape[1], -1)


def make_shards(chan_axes, reduce_order):
    def shards(spectra, sources):
        whitened = whiten(spectra)
        regrouped = lax.all_to_all(whitened, "seg", split_axis=2, concat_axis=1, tiled=True)
        ch_dev = spectra.shape[2]
        freqs = spectra.shape[3]
        first_row = lax.axis_index(chan_axes) * ch_dev
        lag_table = lag_matrix(freqs, LAGS)
        local_row = sources.reshape(-1) - first_row
        onehot = (local_row[:, None] == jnp.arange(ch_dev, dtype=jnp.int32)[None, :]).astype(
            jnp.bfloat16
        )
        local_spec = jnp.einsum(
            "pc,xscf->xpsf", onehot, whitened, preferred_element_type=jnp.float32
        ).astype(jnp.bfloat16)
        for axis in reduce_order:
            local_spec = lax.psum(local_spec, axis)
        source_spec = lax.all_gather(local_spec, "seg", axis=2, tiled=True)
        return correlate(source_spec, regrouped, lag_table)

    return shards


def solution(mesh):
    chan = mesh.shape["chan"]
    sizes = tuple(size for _, size in CHAN_FACTORS)
    if math.prod(sizes) == chan:
        devices = mesh.devices.reshape(sizes + (mesh.shape["seg"],))
        fine = Mesh(devices, CHAN_AXES + ("seg",))
        chan_axes, reduce_order = CHAN_AXES, REDUCE_ORDER
    else:
        fine = mesh
        chan_axes, reduce_order = "chan", ("chan",)
    placed = (P(None, "seg", chan_axes, None), P())
    return jax.shard_map(
        make_shards(chan_axes, reduce_order),
        mesh=fine,
        in_specs=placed,
        out_specs=P(None, tuple(chan_axes) + ("seg",) if isinstance(chan_axes, tuple) else ("chan", "seg"), None),
        check_vma=False,
    )
```

```python
import math

import jax
import jax.numpy as jnp
from jax import lax
from jax.sharding import Mesh, PartitionSpec as P

LAGS = 256
CHAN_FACTORS = (("x", 4), ("zh", 2), ("y", 8), ("c", 2))
CHAN_AXES = tuple(name for name, _ in CHAN_FACTORS)
REDUCE_ORDER = (("c", 2), ("y", 8), ("zh", 2), ("x", 4))


def whiten(spectra):
    values = spectra.astype(jnp.float32)
    power_mean = jnp.mean(values[0] * values[0] + values[1] * values[1], axis=-1)
    inv_scale = lax.rsqrt(power_mean + 1e-06)
    return (values * inv_scale[None, :, :, None]).astype(jnp.bfloat16)


def lag_matrix(freqs, half_lags):
    period = 2 * freqs
    rows = jnp.arange(freqs, dtype=jnp.int32)
    shifts = jnp.arange(2 * half_lags, dtype=jnp.int32) - half_lags
    phase = jnp.mod(rows[:, None] * shifts[None, :], period)
    angles = phase.astype(jnp.float32) * (2.0 * math.pi / period)
    return jnp.concatenate([jnp.cos(angles), -jnp.sin(angles)], axis=0)


def correlate(source_spec, receiver_spec, lag_table):
    segs = receiver_spec.shape[1]
    freqs = receiver_spec.shape[3]
    real_part = jnp.einsum(
        "pkf,krf->prf", source_spec[0], receiver_spec[0], preferred_element_type=jnp.float32
    ) + jnp.einsum(
        "pkf,krf->prf", source_spec[1], receiver_spec[1], preferred_element_type=jnp.float32
    )
    imag_part = jnp.einsum(
        "pkf,krf->prf", source_spec[0], receiver_spec[1], preferred_element_type=jnp.float32
    ) - jnp.einsum(
        "pkf,krf->prf", source_spec[1], receiver_spec[0], preferred_element_type=jnp.float32
    )
    stacked = jnp.concatenate([real_part, imag_part], axis=-1) * (1.0 / math.sqrt(segs))
    flat = stacked.reshape(-1, 2 * freqs)
    result = jnp.dot(
        flat, lag_table, precision=lax.Precision.HIGHEST, preferred_element_type=jnp.float32
    ) * (1.0 / math.sqrt(freqs))
    return result.reshape(stacked.shape[0], stacked.shape[1], -1)


def exchange_sum(value, axis, size):
    if size & (size - 1):
        return lax.psum(value, axis)
    step = 1
    while step < size:
        pairs = [(i, i ^ step) for i in range(size)]
        value = value + lax.ppermute(value, axis, pairs)
        step *= 2
    return value


def make_shards(chan_axes, reduce_order):
    def shards(spectra, sources):
        whitened = whiten(spectra)
        regrouped = lax.all_to_all(whitened, "seg", split_axis=2, concat_axis=1, tiled=True)
        ch_dev = spectra.shape[2]
        freqs = spectra.shape[3]
        first_row = lax.axis_index(chan_axes) * ch_dev
        lag_table = lag_matrix(freqs, LAGS)
        local_row = sources.reshape(-1) - first_row
        onehot = (local_row[:, None] == jnp.arange(ch_dev, dtype=jnp.int32)[None, :]).astype(
            jnp.bfloat16
        )
        local_spec = jnp.einsum(
            "pc,xscf->xpsf", onehot, whitened, preferred_element_type=jnp.float32
        ).astype(jnp.bfloat16)
        for axis, size in reduce_order:
            local_spec = exchange_sum(local_spec, axis, size)
        source_spec = lax.all_gather(local_spec, "seg", axis=2, tiled=True)
        return correlate(source_spec, regrouped, lag_table)

    return shards


def solution(mesh):
    chan = mesh.shape["chan"]
    sizes = tuple(size for _, size in CHAN_FACTORS)
    if math.prod(sizes) == chan:
        devices = mesh.devices.reshape(sizes + (mesh.shape["seg"],))
        fine = Mesh(devices, CHAN_AXES + ("seg",))
        chan_axes, reduce_order = CHAN_AXES, REDUCE_ORDER
    else:
        fine = mesh
        chan_axes, reduce_order = "chan", (("chan", chan),)
    placed = (P(None, "seg", chan_axes, None), P())
    return jax.shard_map(
        make_shards(chan_axes, reduce_order),
        mesh=fine,
        in_specs=placed,
        out_specs=P(None, tuple(chan_axes) + ("seg",) if isinstance(chan_axes, tuple) else ("chan", "seg"), None),
        check_vma=False,
    )
```

```python
import math

import jax
import jax.numpy as jnp
from jax import lax
from jax.sharding import Mesh, PartitionSpec as P

LAGS = 256
CHAN_FACTORS = (("x", 4), ("zh", 2), ("y", 8), ("c", 2))
CHAN_AXES = tuple(name for name, _ in CHAN_FACTORS)
REDUCE_STEPS = (("c", 2, 1), ("y", 8, 1), ("x", 4, 1), ("y", 8, 2), ("x", 4, 2), ("zh", 2, 1), ("y", 8, 4))


def whiten(spectra):
    values = spectra.astype(jnp.float32)
    power_mean = jnp.mean(values[0] * values[0] + values[1] * values[1], axis=-1)
    inv_scale = lax.rsqrt(power_mean + 1e-06)
    return (values * inv_scale[None, :, :, None]).astype(jnp.bfloat16)


def lag_matrix(freqs, half_lags):
    period = 2 * freqs
    rows = jnp.arange(freqs, dtype=jnp.int32)
    shifts = jnp.arange(2 * half_lags, dtype=jnp.int32) - half_lags
    phase = jnp.mod(rows[:, None] * shifts[None, :], period)
    angles = phase.astype(jnp.float32) * (2.0 * math.pi / period)
    return jnp.concatenate([jnp.cos(angles), -jnp.sin(angles)], axis=0)


def correlate(source_spec, receiver_spec, lag_table):
    segs = receiver_spec.shape[1]
    freqs = receiver_spec.shape[3]
    real_part = jnp.einsum(
        "pkf,krf->prf", source_spec[0], receiver_spec[0], preferred_element_type=jnp.float32
    ) + jnp.einsum(
        "pkf,krf->prf", source_spec[1], receiver_spec[1], preferred_element_type=jnp.float32
    )
    imag_part = jnp.einsum(
        "pkf,krf->prf", source_spec[0], receiver_spec[1], preferred_element_type=jnp.float32
    ) - jnp.einsum(
        "pkf,krf->prf", source_spec[1], receiver_spec[0], preferred_element_type=jnp.float32
    )
    stacked = jnp.concatenate([real_part, imag_part], axis=-1) * (1.0 / math.sqrt(segs))
    flat = stacked.reshape(-1, 2 * freqs)
    result = jnp.dot(
        flat, lag_table, precision=lax.Precision.HIGHEST, preferred_element_type=jnp.float32
    ) * (1.0 / math.sqrt(freqs))
    return result.reshape(stacked.shape[0], stacked.shape[1], -1)


def halving_steps(chan_order):
    steps = []
    for axis, size in chan_order:
        bit = 1
        while bit < size:
            steps.append((axis, size, bit))
            bit *= 2
    return steps


def chan_allreduce(value, steps):
    rows = value.shape[0]
    pieces = []
    for axis, size, bit in steps:
        mine = (lax.axis_index(axis) // bit) % 2 == 1
        half = value.shape[0] // 2
        low, high = value[:half], value[half:]
        keep = jnp.where(mine, high, low)
        send = jnp.where(mine, low, high)
        pairs = [(i, i ^ bit) for i in range(size)]
        value = keep + lax.ppermute(send, axis, pairs)
        pieces.append((axis, size, bit, mine))
    for axis, size, bit, mine in reversed(pieces):
        pairs = [(i, i ^ bit) for i in range(size)]
        other = lax.ppermute(value, axis, pairs)
        value = jnp.concatenate(
            [jnp.where(mine, other, value), jnp.where(mine, value, other)], axis=0
        )
    assert value.shape[0] == rows
    return value


def make_shards(chan_axes, reduce_order):
    def shards(spectra, sources):
        whitened = whiten(spectra)
        regrouped = lax.all_to_all(whitened, "seg", split_axis=2, concat_axis=1, tiled=True)
        ch_dev = spectra.shape[2]
        freqs = spectra.shape[3]
        first_row = lax.axis_index(chan_axes) * ch_dev
        lag_table = lag_matrix(freqs, LAGS)
        local_row = sources.reshape(-1) - first_row
        onehot = (local_row[:, None] == jnp.arange(ch_dev, dtype=jnp.int32)[None, :]).astype(
            jnp.bfloat16
        )
        local_spec = jnp.einsum(
            "pc,xscf->xpsf", onehot, whitened, preferred_element_type=jnp.float32
        ).astype(jnp.bfloat16)
        shape = local_spec.shape
        steps = reduce_order
        local_spec = chan_allreduce(local_spec.reshape(-1, shape[-1]), steps).reshape(shape)
        source_spec = lax.all_gather(local_spec, "seg", axis=2, tiled=True)
        return correlate(source_spec, regrouped, lag_table)

    return shards


def solution(mesh):
    chan = mesh.shape["chan"]
    sizes = tuple(size for _, size in CHAN_FACTORS)
    if math.prod(sizes) == chan:
        devices = mesh.devices.reshape(sizes + (mesh.shape["seg"],))
        fine = Mesh(devices, CHAN_AXES + ("seg",))
        chan_axes, reduce_order = CHAN_AXES, REDUCE_STEPS
    else:
        fine = mesh
        chan_axes, reduce_order = "chan", halving_steps((("chan", chan),))
    placed = (P(None, "seg", chan_axes, None), P())
    return jax.shard_map(
        make_shards(chan_axes, reduce_order),
        mesh=fine,
        in_specs=placed,
        out_specs=P(None, tuple(chan_axes) + ("seg",) if isinstance(chan_axes, tuple) else ("chan", "seg"), None),
        check_vma=False,
    )
```

```python
import math

import jax
import jax.numpy as jnp
from jax import lax
from jax.sharding import Mesh, PartitionSpec as P

LAGS = 256
CHAN_FACTORS = (("x", 4), ("zh", 2), ("y", 8), ("c", 2))
CHAN_AXES = tuple(name for name, _ in CHAN_FACTORS)
REDUCE_STEPS = (("c", 2, 1), ("y", 8, 1), ("x", 4, 1), ("y", 8, 2), ("x", 4, 2), ("zh", 2, 1), ("y", 8, 4))


def whiten(spectra):
    values = spectra.astype(jnp.float32)
    power_mean = jnp.mean(values[0] * values[0] + values[1] * values[1], axis=-1)
    inv_scale = lax.rsqrt(power_mean + 1e-06)
    return (values * inv_scale[None, :, :, None]).astype(jnp.bfloat16)


def lag_matrix(freqs, half_lags):
    period = 2 * freqs
    rows = jnp.arange(freqs, dtype=jnp.int32)
    shifts = jnp.arange(2 * half_lags, dtype=jnp.int32) - half_lags
    phase = jnp.mod(rows[:, None] * shifts[None, :], period)
    angles = phase.astype(jnp.float32) * (2.0 * math.pi / period)
    return jnp.concatenate([jnp.cos(angles), -jnp.sin(angles)], axis=0)


def correlate(source_spec, receiver_spec, lag_table):
    segs = receiver_spec.shape[1]
    freqs = receiver_spec.shape[3]
    real_part = jnp.einsum(
        "pkf,krf->prf", source_spec[0], receiver_spec[0], preferred_element_type=jnp.float32
    ) + jnp.einsum(
        "pkf,krf->prf", source_spec[1], receiver_spec[1], preferred_element_type=jnp.float32
    )
    imag_part = jnp.einsum(
        "pkf,krf->prf", source_spec[0], receiver_spec[1], preferred_element_type=jnp.float32
    ) - jnp.einsum(
        "pkf,krf->prf", source_spec[1], receiver_spec[0], preferred_element_type=jnp.float32
    )
    stacked = jnp.concatenate([real_part, imag_part], axis=-1) * (1.0 / math.sqrt(segs))
    flat = stacked.reshape(-1, 2 * freqs)
    result = jnp.dot(
        flat, lag_table, precision=lax.Precision.HIGHEST, preferred_element_type=jnp.float32
    ) * (1.0 / math.sqrt(freqs))
    return result.reshape(stacked.shape[0], stacked.shape[1], -1)


def halving_steps(chan_order):
    steps = []
    for axis, size in chan_order:
        bit = 1
        while bit < size:
            steps.append((axis, size, bit))
            bit *= 2
    return steps


def chan_allreduce(value, steps):
    rows = value.shape[0]
    pieces = []
    for axis, size, bit in steps:
        mine = (lax.axis_index(axis) // bit) % 2 == 1
        half = value.shape[0] // 2
        low, high = value[:half], value[half:]
        keep = jnp.where(mine, high, low)
        send = jnp.where(mine, low, high)
        pairs = [(i, i ^ bit) for i in range(size)]
        value = keep + lax.ppermute(send, axis, pairs)
        pieces.append((axis, size, bit, mine))
    for axis, size, bit, mine in reversed(pieces):
        pairs = [(i, i ^ bit) for i in range(size)]
        other = lax.ppermute(value, axis, pairs)
        value = jnp.concatenate(
            [jnp.where(mine, other, value), jnp.where(mine, value, other)], axis=0
        )
    assert value.shape[0] == rows
    return value


def chan_exchange(value, axes):
    count = lax.psum(1, axes)
    chunks = value.reshape((count, -1) + value.shape[1:])
    mine = lax.all_to_all(chunks, axes, 0, 0).sum(axis=0, dtype=value.dtype)
    spread = jnp.broadcast_to(mine[None], chunks.shape)
    return lax.all_to_all(spread, axes, 0, 0).reshape(value.shape)


def make_shards(chan_axes, reduce_order):
    def shards(spectra, sources):
        whitened = whiten(spectra)
        regrouped = lax.all_to_all(whitened, "seg", split_axis=2, concat_axis=1, tiled=True)
        ch_dev = spectra.shape[2]
        freqs = spectra.shape[3]
        first_row = lax.axis_index(chan_axes) * ch_dev
        lag_table = lag_matrix(freqs, LAGS)
        local_row = sources.reshape(-1) - first_row
        onehot = (local_row[:, None] == jnp.arange(ch_dev, dtype=jnp.int32)[None, :]).astype(
            jnp.bfloat16
        )
        local_spec = jnp.einsum(
            "pc,xscf->xpsf", onehot, whitened, preferred_element_type=jnp.float32
        ).astype(jnp.bfloat16)
        shape = local_spec.shape
        local_spec = chan_exchange(local_spec.reshape(-1, shape[-1]), chan_axes).reshape(shape)
        source_spec = lax.all_gather(local_spec, "seg", axis=2, tiled=True)
        return correlate(source_spec, regrouped, lag_table)

    return shards


def solution(mesh):
    chan = mesh.shape["chan"]
    sizes = tuple(size for _, size in CHAN_FACTORS)
    if math.prod(sizes) == chan:
        devices = mesh.devices.reshape(sizes + (mesh.shape["seg"],))
        fine = Mesh(devices, CHAN_AXES + ("seg",))
        chan_axes, reduce_order = CHAN_AXES, REDUCE_STEPS
    else:
        fine = mesh
        chan_axes, reduce_order = "chan", halving_steps((("chan", chan),))
    placed = (P(None, "seg", chan_axes, None), P())
    return jax.shard_map(
        make_shards(chan_axes, reduce_order),
        mesh=fine,
        in_specs=placed,
        out_specs=P(None, tuple(chan_axes) + ("seg",) if isinstance(chan_axes, tuple) else ("chan", "seg"), None),
        check_vma=False,
    )
```

```python
import math

import jax
import jax.numpy as jnp
from jax import lax
from jax.sharding import Mesh, PartitionSpec as P

LAGS = 256
CHAN_FACTORS = (("x", 4), ("zh", 2), ("y", 8), ("c", 2))
CHAN_AXES = tuple(name for name, _ in CHAN_FACTORS)


def whiten(spectra):
    values = spectra.astype(jnp.float32)
    power_mean = jnp.mean(values[0] * values[0] + values[1] * values[1], axis=-1)
    inv_scale = lax.rsqrt(power_mean + 1e-06)
    return (values * inv_scale[None, :, :, None]).astype(jnp.bfloat16)


def lag_matrix(freqs, half_lags):
    period = 2 * freqs
    rows = jnp.arange(freqs, dtype=jnp.int32)
    shifts = jnp.arange(2 * half_lags, dtype=jnp.int32) - half_lags
    phase = jnp.mod(rows[:, None] * shifts[None, :], period)
    angles = phase.astype(jnp.float32) * (2.0 * math.pi / period)
    return jnp.concatenate([jnp.cos(angles), -jnp.sin(angles)], axis=0)


def correlate(source_spec, receiver_spec, lag_table):
    segs = receiver_spec.shape[1]
    freqs = receiver_spec.shape[3]
    real_part = jnp.einsum(
        "pkf,krf->prf", source_spec[0], receiver_spec[0], preferred_element_type=jnp.float32
    ) + jnp.einsum(
        "pkf,krf->prf", source_spec[1], receiver_spec[1], preferred_element_type=jnp.float32
    )
    imag_part = jnp.einsum(
        "pkf,krf->prf", source_spec[0], receiver_spec[1], preferred_element_type=jnp.float32
    ) - jnp.einsum(
        "pkf,krf->prf", source_spec[1], receiver_spec[0], preferred_element_type=jnp.float32
    )
    stacked = jnp.concatenate([real_part, imag_part], axis=-1) * (1.0 / math.sqrt(segs))
    flat = stacked.reshape(-1, 2 * freqs)
    result = jnp.dot(
        flat, lag_table, precision=lax.Precision.HIGHEST, preferred_element_type=jnp.float32
    ) * (1.0 / math.sqrt(freqs))
    return result.reshape(stacked.shape[0], stacked.shape[1], -1)


def gather_sources(value, chan_axes, seg_axis):
    parts, sources, local_segs, freqs = value.shape
    count = lax.psum(1, chan_axes)
    segs = lax.psum(1, seg_axis)
    chunks = value.reshape(count, -1, freqs)
    rows = chunks.shape[1]
    mine = lax.all_to_all(chunks, chan_axes, 0, 0).sum(axis=0, dtype=value.dtype)
    spread = jnp.broadcast_to(mine[None], (count * segs, rows, freqs))
    got = lax.all_to_all(spread, chan_axes + (seg_axis,), 0, 0)
    split = local_segs // rows
    got = got.reshape(parts, sources, split, segs, rows, freqs).transpose(0, 1, 3, 2, 4, 5)
    return got.reshape(parts, sources, segs * local_segs, freqs)


def make_shards(chan_axes):
    def shards(spectra, sources):
        whitened = whiten(spectra)
        regrouped = lax.all_to_all(whitened, "seg", split_axis=2, concat_axis=1, tiled=True)
        ch_dev = spectra.shape[2]
        freqs = spectra.shape[3]
        first_row = lax.axis_index(chan_axes) * ch_dev
        lag_table = lag_matrix(freqs, LAGS)
        local_row = sources.reshape(-1) - first_row
        onehot = (local_row[:, None] == jnp.arange(ch_dev, dtype=jnp.int32)[None, :]).astype(
            jnp.bfloat16
        )
        local_spec = jnp.einsum(
            "pc,xscf->xpsf", onehot, whitened, preferred_element_type=jnp.float32
        ).astype(jnp.bfloat16)
        source_spec = gather_sources(local_spec, chan_axes, "seg")
        return correlate(source_spec, regrouped, lag_table)

    return shards


def solution(mesh):
    chan = mesh.shape["chan"]
    sizes = tuple(size for _, size in CHAN_FACTORS)
    if math.prod(sizes) == chan:
        devices = mesh.devices.reshape(sizes + (mesh.shape["seg"],))
        fine = Mesh(devices, CHAN_AXES + ("seg",))
        chan_axes = CHAN_AXES
    else:
        fine = mesh
        chan_axes = ("chan",)
    placed = (P(None, "seg", chan_axes, None), P())
    return jax.shard_map(
        make_shards(chan_axes),
        mesh=fine,
        in_specs=placed,
        out_specs=P(None, chan_axes + ("seg",), None),
        check_vma=False,
    )
```

```python
import math

import jax
import jax.numpy as jnp
from jax import lax
from jax.sharding import Mesh, PartitionSpec as P

LAGS = 256
CHAN_FACTORS = (("x", 4), ("zh", 2), ("y", 8), ("c", 2))
CHAN_AXES = tuple(name for name, _ in CHAN_FACTORS)


def whiten(spectra):
    values = spectra.astype(jnp.float32)
    power_mean = jnp.mean(values[0] * values[0] + values[1] * values[1], axis=-1)
    inv_scale = lax.rsqrt(power_mean + 1e-06)
    return (values * inv_scale[None, :, :, None]).astype(jnp.bfloat16)


def lag_matrix(freqs, half_lags):
    period = 2 * freqs
    rows = jnp.arange(freqs, dtype=jnp.int32)
    shifts = jnp.arange(2 * half_lags, dtype=jnp.int32) - half_lags
    phase = jnp.mod(rows[:, None] * shifts[None, :], period)
    angles = phase.astype(jnp.float32) * (2.0 * math.pi / period)
    return jnp.concatenate([jnp.cos(angles), -jnp.sin(angles)], axis=0)


def correlate(source_spec, receiver_spec, lag_table):
    segs = receiver_spec.shape[1]
    freqs = receiver_spec.shape[3]
    a = source_spec[0].astype(jnp.float32)[:, :, None, :]
    b = source_spec[1].astype(jnp.float32)[:, :, None, :]
    c = receiver_spec[0].astype(jnp.float32)[:, None, :, :]
    d = receiver_spec[1].astype(jnp.float32)[:, None, :, :]
    real_part = jnp.sum(a * c + b * d, axis=0)
    imag_part = jnp.sum(a * d - b * c, axis=0)
    stacked = jnp.concatenate([real_part, imag_part], axis=-1) * (1.0 / math.sqrt(segs))
    flat = stacked.reshape(-1, 2 * freqs)
    result = jnp.dot(
        flat, lag_table, precision=lax.Precision.HIGHEST, preferred_element_type=jnp.float32
    ) * (1.0 / math.sqrt(freqs))
    return result.reshape(stacked.shape[0], stacked.shape[1], -1)


def gather_sources(value, chan_axes, seg_axis):
    parts, sources, local_segs, freqs = value.shape
    count = lax.psum(1, chan_axes)
    segs = lax.psum(1, seg_axis)
    chunks = value.reshape(count, -1, freqs)
    rows = chunks.shape[1]
    mine = lax.all_to_all(chunks, chan_axes, 0, 0).sum(axis=0, dtype=value.dtype)
    spread = jnp.broadcast_to(mine[None], (count * segs, rows, freqs))
    got = lax.all_to_all(spread, chan_axes + (seg_axis,), 0, 0)
    split = local_segs // rows
    got = got.reshape(parts, sources, split, segs, rows, freqs).transpose(0, 3, 2, 4, 1, 5)
    return got.reshape(parts, segs * local_segs, sources, freqs)


def make_shards(chan_axes):
    def shards(spectra, sources):
        whitened = whiten(spectra)
        regrouped = lax.all_to_all(whitened, "seg", split_axis=2, concat_axis=1, tiled=True)
        ch_dev = spectra.shape[2]
        freqs = spectra.shape[3]
        first_row = lax.axis_index(chan_axes) * ch_dev
        lag_table = lag_matrix(freqs, LAGS)
        local_row = sources.reshape(-1) - first_row
        onehot = (local_row[:, None] == jnp.arange(ch_dev, dtype=jnp.int32)[None, :]).astype(
            jnp.bfloat16
        )
        local_spec = jnp.einsum(
            "pc,xscf->xpsf", onehot, whitened, preferred_element_type=jnp.float32
        ).astype(jnp.bfloat16)
        source_spec = gather_sources(local_spec, chan_axes, "seg")
        return correlate(source_spec, regrouped, lag_table)

    return shards


def solution(mesh):
    chan = mesh.shape["chan"]
    sizes = tuple(size for _, size in CHAN_FACTORS)
    if math.prod(sizes) == chan:
        devices = mesh.devices.reshape(sizes + (mesh.shape["seg"],))
        fine = Mesh(devices, CHAN_AXES + ("seg",))
        chan_axes = CHAN_AXES
    else:
        fine = mesh
        chan_axes = ("chan",)
    placed = (P(None, "seg", chan_axes, None), P())
    return jax.shard_map(
        make_shards(chan_axes),
        mesh=fine,
        in_specs=placed,
        out_specs=P(None, chan_axes + ("seg",), None),
        check_vma=False,
    )
```

```python
import math

import jax
import jax.numpy as jnp
from jax import lax
from jax.sharding import Mesh, PartitionSpec as P

LAGS = 256
CHAN_FACTORS = (("x", 4), ("zh", 2), ("y", 8), ("c", 2))
CHAN_AXES = tuple(name for name, _ in CHAN_FACTORS)


def whiten(spectra):
    values = spectra.astype(jnp.float32)
    power_mean = jnp.mean(values[0] * values[0] + values[1] * values[1], axis=-1)
    inv_scale = lax.rsqrt(power_mean + 1e-06)
    return (values * inv_scale[None, :, :, None]).astype(jnp.bfloat16)


def lag_matrix(freqs, half_lags):
    period = 2 * freqs
    rows = jnp.arange(freqs, dtype=jnp.int32)
    shifts = jnp.arange(2 * half_lags, dtype=jnp.int32) - half_lags
    phase = jnp.mod(rows[:, None] * shifts[None, :], period)
    angles = phase.astype(jnp.float32) * (2.0 * math.pi / period)
    return jnp.concatenate([jnp.cos(angles), -jnp.sin(angles)], axis=0)


def correlate(source_spec, receiver_spec, lag_table):
    segs = receiver_spec.shape[1]
    freqs = receiver_spec.shape[3]
    a = source_spec[0].astype(jnp.float32)[:, :, None, :]
    b = source_spec[1].astype(jnp.float32)[:, :, None, :]
    c = receiver_spec[0].astype(jnp.float32)[:, None, :, :]
    d = receiver_spec[1].astype(jnp.float32)[:, None, :, :]
    real_part = jnp.sum(a * c + b * d, axis=0)
    imag_part = jnp.sum(a * d - b * c, axis=0)
    stacked = jnp.concatenate([real_part, imag_part], axis=-1) * (1.0 / math.sqrt(segs))
    flat = stacked.reshape(-1, 2 * freqs)
    result = jnp.dot(
        flat, lag_table, precision=lax.Precision.HIGHEST, preferred_element_type=jnp.float32
    ) * (1.0 / math.sqrt(freqs))
    return result.reshape(stacked.shape[0], stacked.shape[1], -1)


def gather_sources(value, chan_axes, seg_axis):
    parts, sources, local_segs, freqs = value.shape
    count = lax.psum(1, chan_axes)
    segs = lax.psum(1, seg_axis)
    chunks = value.reshape(count, -1, freqs)
    rows = chunks.shape[1]
    if chan_axes == CHAN_AXES:
        inner = lax.psum(1, ("y", "c"))
        outer = count // inner
        part = value.reshape(inner, -1, freqs)
        part = lax.all_to_all(part, ("y", "c"), 0, 0).sum(axis=0, dtype=value.dtype)
        part = part.reshape(outer, rows, freqs)
        mine = lax.all_to_all(part, ("x", "zh"), 0, 0).sum(axis=0, dtype=value.dtype)
    else:
        mine = lax.all_to_all(chunks, chan_axes, 0, 0).sum(axis=0, dtype=value.dtype)
    spread = jnp.broadcast_to(mine[None], (count * segs, rows, freqs))
    got = lax.all_to_all(spread, chan_axes + (seg_axis,), 0, 0)
    if chan_axes == CHAN_AXES:
        got = got.reshape(outer, inner, segs, rows, freqs).transpose(1, 0, 2, 3, 4)
    split = local_segs // rows
    got = got.reshape(parts, sources, split, segs, rows, freqs).transpose(0, 3, 2, 4, 1, 5)
    return got.reshape(parts, segs * local_segs, sources, freqs)


def make_shards(chan_axes):
    def shards(spectra, sources):
        whitened = whiten(spectra)
        regrouped = lax.all_to_all(whitened, "seg", split_axis=2, concat_axis=1, tiled=True)
        ch_dev = spectra.shape[2]
        freqs = spectra.shape[3]
        first_row = lax.axis_index(chan_axes) * ch_dev
        lag_table = lag_matrix(freqs, LAGS)
        local_row = sources.reshape(-1) - first_row
        onehot = (local_row[:, None] == jnp.arange(ch_dev, dtype=jnp.int32)[None, :]).astype(
            jnp.bfloat16
        )
        local_spec = jnp.einsum(
            "pc,xscf->xpsf", onehot, whitened, preferred_element_type=jnp.float32
        ).astype(jnp.bfloat16)
        source_spec = gather_sources(local_spec, chan_axes, "seg")
        return correlate(source_spec, regrouped, lag_table)

    return shards


def solution(mesh):
    chan = mesh.shape["chan"]
    sizes = tuple(size for _, size in CHAN_FACTORS)
    if math.prod(sizes) == chan:
        devices = mesh.devices.reshape(sizes + (mesh.shape["seg"],))
        fine = Mesh(devices, CHAN_AXES + ("seg",))
        chan_axes = CHAN_AXES
    else:
        fine = mesh
        chan_axes = ("chan",)
    placed = (P(None, "seg", chan_axes, None), P())
    return jax.shard_map(
        make_shards(chan_axes),
        mesh=fine,
        in_specs=placed,
        out_specs=P(None, chan_axes + ("seg",), None),
        check_vma=False,
    )
```

```python
import math

import jax
import jax.numpy as jnp
from jax import lax
from jax.sharding import Mesh, PartitionSpec as P

LAGS = 256
CHAN_FACTORS = (("x", 4), ("zh", 2), ("y", 8), ("c", 2))
CHAN_AXES = tuple(name for name, _ in CHAN_FACTORS)


def whiten(spectra):
    values = spectra.astype(jnp.float32)
    power_mean = jnp.mean(values[0] * values[0] + values[1] * values[1], axis=-1)
    inv_scale = lax.rsqrt(power_mean + 1e-06)
    return (values * inv_scale[None, :, :, None]).astype(jnp.bfloat16)


def lag_matrix(freqs, half_lags):
    period = 2 * freqs
    rows = jnp.arange(freqs, dtype=jnp.int32)
    shifts = jnp.arange(2 * half_lags, dtype=jnp.int32) - half_lags
    phase = jnp.mod(rows[:, None] * shifts[None, :], period)
    angles = phase.astype(jnp.float32) * (2.0 * math.pi / period)
    return jnp.concatenate([jnp.cos(angles), -jnp.sin(angles)], axis=0)


def correlate(source_spec, receiver_spec, lag_table):
    segs = receiver_spec.shape[1]
    freqs = receiver_spec.shape[3]
    a = source_spec[0].astype(jnp.float32)[:, :, None, :]
    b = source_spec[1].astype(jnp.float32)[:, :, None, :]
    c = receiver_spec[0].astype(jnp.float32)[:, None, :, :]
    d = receiver_spec[1].astype(jnp.float32)[:, None, :, :]
    real_part = jnp.sum(a * c + b * d, axis=0)
    imag_part = jnp.sum(a * d - b * c, axis=0)
    stacked = jnp.concatenate([real_part, imag_part], axis=-1) * (1.0 / math.sqrt(segs))
    flat = stacked.reshape(-1, 2 * freqs)
    result = jnp.dot(
        flat, lag_table, precision=lax.Precision.HIGHEST, preferred_element_type=jnp.float32
    ) * (1.0 / math.sqrt(freqs))
    return result.reshape(stacked.shape[0], stacked.shape[1], -1)


def gather_sources(value, chan_axes, seg_axis):
    parts, sources, local_segs, freqs = value.shape
    count = lax.psum(1, chan_axes)
    segs = lax.psum(1, seg_axis)
    chunks = value.reshape(count, -1, freqs)
    rows = chunks.shape[1]
    mine = lax.all_to_all(chunks, chan_axes, 0, 0).sum(axis=0, dtype=value.dtype)
    got = lax.all_gather(mine, chan_axes + (seg_axis,), axis=0)
    split = local_segs // rows
    got = got.reshape(parts, sources, split, segs, rows, freqs).transpose(0, 3, 2, 4, 1, 5)
    return got.reshape(parts, segs * local_segs, sources, freqs)


def make_shards(chan_axes):
    def shards(spectra, sources):
        whitened = whiten(spectra)
        regrouped = lax.all_to_all(whitened, "seg", split_axis=2, concat_axis=1, tiled=True)
        ch_dev = spectra.shape[2]
        freqs = spectra.shape[3]
        first_row = lax.axis_index(chan_axes) * ch_dev
        lag_table = lag_matrix(freqs, LAGS)
        local_row = sources.reshape(-1) - first_row
        onehot = (local_row[:, None] == jnp.arange(ch_dev, dtype=jnp.int32)[None, :]).astype(
            jnp.bfloat16
        )
        local_spec = jnp.einsum(
            "pc,xscf->xpsf", onehot, whitened, preferred_element_type=jnp.float32
        ).astype(jnp.bfloat16)
        source_spec = gather_sources(local_spec, chan_axes, "seg")
        return correlate(source_spec, regrouped, lag_table)

    return shards


def solution(mesh):
    chan = mesh.shape["chan"]
    sizes = tuple(size for _, size in CHAN_FACTORS)
    if math.prod(sizes) == chan:
        devices = mesh.devices.reshape(sizes + (mesh.shape["seg"],))
        fine = Mesh(devices, CHAN_AXES + ("seg",))
        chan_axes = CHAN_AXES
    else:
        fine = mesh
        chan_axes = ("chan",)
    placed = (P(None, "seg", chan_axes, None), P())
    return jax.shard_map(
        make_shards(chan_axes),
        mesh=fine,
        in_specs=placed,
        out_specs=P(None, chan_axes + ("seg",), None),
        check_vma=False,
    )
```

```python
import math

import jax
import jax.numpy as jnp
from jax import lax
from jax.sharding import Mesh, PartitionSpec as P

LAGS = 256
CHAN_FACTORS = (("x", 4), ("zh", 2), ("y", 8), ("c", 2))
CHAN_AXES = tuple(name for name, _ in CHAN_FACTORS)


def whiten(spectra):
    values = spectra.astype(jnp.float32)
    power_mean = jnp.mean(values[0] * values[0] + values[1] * values[1], axis=-1)
    inv_scale = lax.rsqrt(power_mean + 1e-06)
    return (values * inv_scale[None, :, :, None]).astype(jnp.bfloat16)


def lag_matrix(freqs, half_lags):
    period = 2 * freqs
    rows = jnp.arange(freqs, dtype=jnp.int32)
    shifts = jnp.arange(2 * half_lags, dtype=jnp.int32) - half_lags
    phase = jnp.mod(rows[:, None] * shifts[None, :], period)
    angles = phase.astype(jnp.float32) * (2.0 * math.pi / period)
    return jnp.concatenate([jnp.cos(angles), -jnp.sin(angles)], axis=0)


def correlate(source_spec, receiver_spec, lag_table):
    segs = receiver_spec.shape[1]
    freqs = receiver_spec.shape[3]
    a = source_spec[0].astype(jnp.float32)[:, :, None, :]
    b = source_spec[1].astype(jnp.float32)[:, :, None, :]
    c = receiver_spec[0].astype(jnp.float32)[:, None, :, :]
    d = receiver_spec[1].astype(jnp.float32)[:, None, :, :]
    real_part = jnp.sum(a * c + b * d, axis=0)
    imag_part = jnp.sum(a * d - b * c, axis=0)
    stacked = jnp.concatenate([real_part, imag_part], axis=-1) * (1.0 / math.sqrt(segs))
    flat = stacked.reshape(-1, 2 * freqs)
    result = jnp.dot(
        flat, lag_table, precision=lax.Precision.HIGHEST, preferred_element_type=jnp.float32
    ) * (1.0 / math.sqrt(freqs))
    return result.reshape(stacked.shape[0], stacked.shape[1], -1)


def gather_sources(value, chan_axes, seg_axis):
    parts, sources, local_segs, freqs = value.shape
    count = lax.psum(1, chan_axes)
    segs = lax.psum(1, seg_axis)
    chunks = value.reshape(count, -1, freqs)
    rows = chunks.shape[1]
    mine = lax.all_to_all(chunks, chan_axes, 0, 0).sum(axis=0, dtype=value.dtype)
    spread = jnp.broadcast_to(mine[None], (count * segs, rows, freqs))
    got = lax.all_to_all(spread, chan_axes + (seg_axis,), 0, 0)
    split = local_segs // rows
    got = got.reshape(parts, sources, split, segs, rows, freqs).transpose(0, 3, 2, 4, 1, 5)
    return got.reshape(parts, segs * local_segs, sources, freqs)


def regroup_receivers(whitened, seg_axis):
    segs = lax.psum(1, seg_axis)
    me = lax.axis_index(seg_axis)
    parts, local_segs, ch_dev, freqs = whitened.shape
    groups = whitened.reshape(parts, local_segs, segs, ch_dev // segs, freqs)

    def group(index):
        return lax.dynamic_index_in_dim(groups, index, axis=2, keepdims=False)

    blocks = [group(me)]
    for shift in range(1, segs):
        pairs = [(i, (i + shift) % segs) for i in range(segs)]
        blocks.append(lax.ppermute(group((me + shift) % segs), seg_axis, pairs))
    return jnp.concatenate(blocks[::-1], axis=1)


def rotate_segments(source_spec, seg_axis):
    segs = lax.psum(1, seg_axis)
    me = lax.axis_index(seg_axis)
    parts, all_segs, sources, freqs = source_spec.shape
    doubled = jnp.concatenate([source_spec, source_spec], axis=1)
    return lax.dynamic_slice_in_dim(doubled, ((me + 1) % segs) * (all_segs // segs), all_segs, axis=1)


def make_shards(chan_axes):
    def shards(spectra, sources):
        whitened = whiten(spectra)
        regrouped = regroup_receivers(whitened, "seg")
        ch_dev = spectra.shape[2]
        freqs = spectra.shape[3]
        first_row = lax.axis_index(chan_axes) * ch_dev
        lag_table = lag_matrix(freqs, LAGS)
        local_row = sources.reshape(-1) - first_row
        onehot = (local_row[:, None] == jnp.arange(ch_dev, dtype=jnp.int32)[None, :]).astype(
            jnp.bfloat16
        )
        local_spec = jnp.einsum(
            "pc,xscf->xpsf", onehot, whitened, preferred_element_type=jnp.float32
        ).astype(jnp.bfloat16)
        source_spec = rotate_segments(gather_sources(local_spec, chan_axes, "seg"), "seg")
        return correlate(source_spec, regrouped, lag_table)

    return shards


def solution(mesh):
    chan = mesh.shape["chan"]
    sizes = tuple(size for _, size in CHAN_FACTORS)
    if math.prod(sizes) == chan:
        devices = mesh.devices.reshape(sizes + (mesh.shape["seg"],))
        fine = Mesh(devices, CHAN_AXES + ("seg",))
        chan_axes = CHAN_AXES
    else:
        fine = mesh
        chan_axes = ("chan",)
    placed = (P(None, "seg", chan_axes, None), P())
    return jax.shard_map(
        make_shards(chan_axes),
        mesh=fine,
        in_specs=placed,
        out_specs=P(None, chan_axes + ("seg",), None),
        check_vma=False,
    )
```

```python
import math

import jax
import jax.numpy as jnp
from jax import lax
from jax.sharding import Mesh, PartitionSpec as P

LAGS = 256
CHAN_FACTORS = (("x", 4), ("zh", 2), ("y", 8), ("c", 2))
CHAN_AXES = tuple(name for name, _ in CHAN_FACTORS)


def whiten(spectra):
    values = spectra.astype(jnp.float32)
    power_mean = jnp.mean(values[0] * values[0] + values[1] * values[1], axis=-1)
    inv_scale = lax.rsqrt(power_mean + 1e-06)
    return (values * inv_scale[None, :, :, None]).astype(jnp.bfloat16)


def lag_matrix(freqs, half_lags):
    period = 2 * freqs
    rows = jnp.arange(freqs, dtype=jnp.int32)
    shifts = jnp.arange(2 * half_lags, dtype=jnp.int32) - half_lags
    phase = jnp.mod(rows[:, None] * shifts[None, :], period)
    angles = phase.astype(jnp.float32) * (2.0 * math.pi / period)
    return jnp.concatenate([jnp.cos(angles), -jnp.sin(angles)], axis=0)


def correlate(source_spec, receiver_spec, lag_table):
    segs = receiver_spec.shape[1]
    freqs = receiver_spec.shape[3]
    a = source_spec[0].astype(jnp.float32)[:, :, None, :]
    b = source_spec[1].astype(jnp.float32)[:, :, None, :]
    c = receiver_spec[0].astype(jnp.float32)[:, None, :, :]
    d = receiver_spec[1].astype(jnp.float32)[:, None, :, :]
    real_part = jnp.sum(a * c + b * d, axis=0)
    imag_part = jnp.sum(a * d - b * c, axis=0)
    stacked = jnp.concatenate([real_part, imag_part], axis=-1) * (1.0 / math.sqrt(segs))
    flat = stacked.reshape(-1, 2 * freqs)
    result = jnp.dot(
        flat, lag_table, precision=lax.Precision.HIGHEST, preferred_element_type=jnp.float32
    ) * (1.0 / math.sqrt(freqs))
    return result.reshape(stacked.shape[0], stacked.shape[1], -1)


def gather_sources(value, chan_axes):
    parts, sources, local_segs, freqs = value.shape
    count = lax.psum(1, chan_axes)
    chunks = value.reshape(count, -1, freqs)
    mine = lax.all_to_all(chunks, chan_axes, 0, 0).sum(axis=0, dtype=value.dtype)
    spread = jnp.broadcast_to(mine[None], chunks.shape)
    got = lax.all_to_all(spread, chan_axes, 0, 0).reshape(value.shape)
    return got.transpose(0, 2, 1, 3)


def regroup(whitened, source_spec, seg_axis):
    segs = lax.psum(1, seg_axis)
    me = lax.axis_index(seg_axis)
    parts, local_segs, ch_dev, freqs = whitened.shape
    groups = whitened.reshape(parts, local_segs, segs, ch_dev // segs, freqs)

    def group(index):
        return lax.dynamic_index_in_dim(groups, index, axis=2, keepdims=False)

    receivers = [group(me)]
    sources = [source_spec]
    width = ch_dev // segs
    for shift in range(1, segs):
        pairs = [(i, (i + shift) % segs) for i in range(segs)]
        payload = jnp.concatenate([group((me + shift) % segs), source_spec], axis=2)
        got = lax.ppermute(payload, seg_axis, pairs)
        receivers.append(got[:, :, :width])
        sources.append(got[:, :, width:])
    return jnp.concatenate(sources, axis=1), jnp.concatenate(receivers, axis=1)


def make_shards(chan_axes):
    def shards(spectra, sources):
        whitened = whiten(spectra)
        ch_dev = spectra.shape[2]
        freqs = spectra.shape[3]
        first_row = lax.axis_index(chan_axes) * ch_dev
        lag_table = lag_matrix(freqs, LAGS)
        local_row = sources.reshape(-1) - first_row
        onehot = (local_row[:, None] == jnp.arange(ch_dev, dtype=jnp.int32)[None, :]).astype(
            jnp.bfloat16
        )
        local_spec = jnp.einsum(
            "pc,xscf->xpsf", onehot, whitened, preferred_element_type=jnp.float32
        ).astype(jnp.bfloat16)
        source_spec, regrouped = regroup(whitened, gather_sources(local_spec, chan_axes), "seg")
        return correlate(source_spec, regrouped, lag_table)

    return shards


def solution(mesh):
    chan = mesh.shape["chan"]
    sizes = tuple(size for _, size in CHAN_FACTORS)
    if math.prod(sizes) == chan:
        devices = mesh.devices.reshape(sizes + (mesh.shape["seg"],))
        fine = Mesh(devices, CHAN_AXES + ("seg",))
        chan_axes = CHAN_AXES
    else:
        fine = mesh
        chan_axes = ("chan",)
    placed = (P(None, "seg", chan_axes, None), P())
    return jax.shard_map(
        make_shards(chan_axes),
        mesh=fine,
        in_specs=placed,
        out_specs=P(None, chan_axes + ("seg",), None),
        check_vma=False,
    )
```

```python
import math

import jax
import jax.numpy as jnp
from jax import lax
from jax.sharding import Mesh, PartitionSpec as P

LAGS = 256
CHAN_FACTORS = (("x", 4), ("zh", 2), ("y", 8), ("c", 2))
CHAN_AXES = tuple(name for name, _ in CHAN_FACTORS)


def whiten(spectra):
    values = spectra.astype(jnp.float32)
    power_mean = jnp.mean(values[0] * values[0] + values[1] * values[1], axis=-1)
    inv_scale = lax.rsqrt(power_mean + 1e-06)
    return (values * inv_scale[None, :, :, None]).astype(jnp.bfloat16)


def lag_matrix(freqs, half_lags):
    period = 2 * freqs
    rows = jnp.arange(freqs, dtype=jnp.int32)
    shifts = jnp.arange(2 * half_lags, dtype=jnp.int32) - half_lags
    phase = jnp.mod(rows[:, None] * shifts[None, :], period)
    angles = phase.astype(jnp.float32) * (2.0 * math.pi / period)
    return jnp.concatenate([jnp.cos(angles), -jnp.sin(angles)], axis=0)


def correlate(source_spec, receiver_spec, lag_table):
    segs = receiver_spec.shape[1]
    freqs = receiver_spec.shape[3]
    a = source_spec[0].astype(jnp.float32)[:, :, None, :]
    b = source_spec[1].astype(jnp.float32)[:, :, None, :]
    c = receiver_spec[0].astype(jnp.float32)[:, None, :, :]
    d = receiver_spec[1].astype(jnp.float32)[:, None, :, :]
    real_part = jnp.sum(a * c + b * d, axis=0)
    imag_part = jnp.sum(a * d - b * c, axis=0)
    stacked = jnp.concatenate([real_part, imag_part], axis=-1) * (1.0 / math.sqrt(segs))
    flat = stacked.reshape(-1, 2 * freqs)
    result = jnp.dot(
        flat, lag_table, precision=lax.Precision.HIGHEST, preferred_element_type=jnp.float32
    ) * (1.0 / math.sqrt(freqs))
    return result.reshape(stacked.shape[0], stacked.shape[1], -1)


def gather_sources(value, chan_axes, seg_axis):
    parts, sources, local_segs, freqs = value.shape
    count = lax.psum(1, chan_axes)
    segs = lax.psum(1, seg_axis)
    chunks = value.reshape(count, -1, freqs)
    rows = chunks.shape[1]
    if chan_axes == CHAN_AXES:
        pair = lax.psum(1, "c")
        rest = ("x", "zh", "y")
        upper = lax.axis_index("c") == 1
        flat = value.reshape(pair, -1, freqs)
        keep = jnp.where(upper, flat[1], flat[0])
        send = jnp.where(upper, flat[0], flat[1])
        half = keep + lax.ppermute(send, "c", [(0, 1), (1, 0)])
        part = half.reshape(count // pair, rows, freqs)
        mine = lax.all_to_all(part, rest, 0, 0).sum(axis=0, dtype=value.dtype)
    else:
        mine = lax.all_to_all(chunks, chan_axes, 0, 0).sum(axis=0, dtype=value.dtype)
    spread = jnp.broadcast_to(mine[None], (count * segs, rows, freqs))
    got = lax.all_to_all(spread, chan_axes + (seg_axis,), 0, 0)
    if chan_axes == CHAN_AXES:
        got = got.reshape(count // pair, pair, segs, rows, freqs).transpose(1, 0, 2, 3, 4)
    split = local_segs // rows
    got = got.reshape(parts, sources, split, segs, rows, freqs).transpose(0, 3, 2, 4, 1, 5)
    return got.reshape(parts, segs * local_segs, sources, freqs)


def regroup_receivers(whitened, seg_axis):
    segs = lax.psum(1, seg_axis)
    me = lax.axis_index(seg_axis)
    parts, local_segs, ch_dev, freqs = whitened.shape
    groups = whitened.reshape(parts, local_segs, segs, ch_dev // segs, freqs)

    def group(index):
        return lax.dynamic_index_in_dim(groups, index, axis=2, keepdims=False)

    blocks = [group(me)]
    for shift in range(1, segs):
        pairs = [(i, (i + shift) % segs) for i in range(segs)]
        blocks.append(lax.ppermute(group((me + shift) % segs), seg_axis, pairs))
    return jnp.concatenate(blocks[::-1], axis=1)


def rotate_segments(source_spec, seg_axis):
    segs = lax.psum(1, seg_axis)
    me = lax.axis_index(seg_axis)
    parts, all_segs, sources, freqs = source_spec.shape
    doubled = jnp.concatenate([source_spec, source_spec], axis=1)
    return lax.dynamic_slice_in_dim(doubled, ((me + 1) % segs) * (all_segs // segs), all_segs, axis=1)


def make_shards(chan_axes):
    def shards(spectra, sources):
        whitened = whiten(spectra)
        regrouped = regroup_receivers(whitened, "seg")
        ch_dev = spectra.shape[2]
        freqs = spectra.shape[3]
        first_row = lax.axis_index(chan_axes) * ch_dev
        lag_table = lag_matrix(freqs, LAGS)
        local_row = sources.reshape(-1) - first_row
        onehot = (local_row[:, None] == jnp.arange(ch_dev, dtype=jnp.int32)[None, :]).astype(
            jnp.bfloat16
        )
        local_spec = jnp.einsum(
            "pc,xscf->xpsf", onehot, whitened, preferred_element_type=jnp.float32
        ).astype(jnp.bfloat16)
        source_spec = rotate_segments(gather_sources(local_spec, chan_axes, "seg"), "seg")
        return correlate(source_spec, regrouped, lag_table)

    return shards


def solution(mesh):
    chan = mesh.shape["chan"]
    sizes = tuple(size for _, size in CHAN_FACTORS)
    if math.prod(sizes) == chan:
        devices = mesh.devices.reshape(sizes + (mesh.shape["seg"],))
        fine = Mesh(devices, CHAN_AXES + ("seg",))
        chan_axes = CHAN_AXES
    else:
        fine = mesh
        chan_axes = ("chan",)
    placed = (P(None, "seg", chan_axes, None), P())
    return jax.shard_map(
        make_shards(chan_axes),
        mesh=fine,
        in_specs=placed,
        out_specs=P(None, chan_axes + ("seg",), None),
        check_vma=False,
    )
```

```python
import math

import jax
import jax.numpy as jnp
from jax import lax
from jax.sharding import Mesh, PartitionSpec as P

LAGS = 256
CHAN_FACTORS = (("x", 4), ("zh", 2), ("y", 8), ("c", 2))
CHAN_AXES = tuple(name for name, _ in CHAN_FACTORS)


def whiten(spectra):
    values = spectra.astype(jnp.float32)
    power_mean = jnp.mean(values[0] * values[0] + values[1] * values[1], axis=-1)
    inv_scale = lax.rsqrt(power_mean + 1e-06)
    return (values * inv_scale[None, :, :, None]).astype(jnp.bfloat16)


def lag_matrix(freqs, half_lags):
    period = 2 * freqs
    rows = jnp.arange(freqs, dtype=jnp.int32)
    shifts = jnp.arange(2 * half_lags, dtype=jnp.int32) - half_lags
    phase = jnp.mod(rows[:, None] * shifts[None, :], period)
    angles = phase.astype(jnp.float32) * (2.0 * math.pi / period)
    return jnp.concatenate([jnp.cos(angles), -jnp.sin(angles)], axis=0)


def correlate(source_spec, receiver_spec, lag_table, segs):
    freqs = receiver_spec.shape[3]
    a = source_spec[0].astype(jnp.float32)[:, :, None, :]
    b = source_spec[1].astype(jnp.float32)[:, :, None, :]
    c = receiver_spec[0].astype(jnp.float32)[:, None, :, :]
    d = receiver_spec[1].astype(jnp.float32)[:, None, :, :]
    real_part = jnp.sum(a * c + b * d, axis=0)
    imag_part = jnp.sum(a * d - b * c, axis=0)
    stacked = jnp.concatenate([real_part, imag_part], axis=-1) * (1.0 / math.sqrt(segs))
    flat = stacked.reshape(-1, 2 * freqs)
    result = jnp.dot(
        flat, lag_table, precision=lax.Precision.HIGHEST, preferred_element_type=jnp.float32
    ) * (1.0 / math.sqrt(freqs))
    return result.reshape(stacked.shape[0], stacked.shape[1], -1)


def gather_sources(value, chan_axes):
    parts, sources, local_segs, freqs = value.shape
    count = lax.psum(1, chan_axes)
    rows = value.size // (count * freqs)
    if chan_axes == CHAN_AXES:
        pair = lax.psum(1, "c")
        rest = ("x", "zh", "y")
        upper = lax.axis_index("c") == 1
        flat = value.reshape(pair, -1, freqs)
        keep = jnp.where(upper, flat[1], flat[0])
        send = jnp.where(upper, flat[0], flat[1])
        half = keep + lax.ppermute(send, "c", [(0, 1), (1, 0)])
        part = half.reshape(count // pair, rows, freqs)
        mine = lax.all_to_all(part, rest, 0, 0).sum(axis=0, dtype=value.dtype)
        spread = jnp.broadcast_to(mine[None], (count, rows, freqs))
        got = lax.all_to_all(spread, chan_axes, 0, 0)
        got = got.reshape(count // pair, pair, rows, freqs).transpose(1, 0, 2, 3)
    else:
        chunks = value.reshape(count, rows, freqs)
        mine = lax.all_to_all(chunks, chan_axes, 0, 0).sum(axis=0, dtype=value.dtype)
        spread = jnp.broadcast_to(mine[None], chunks.shape)
        got = lax.all_to_all(spread, chan_axes, 0, 0)
    return got.reshape(value.shape).transpose(0, 2, 1, 3)


def sum_over_seg(partial, seg_axis):
    segs = lax.psum(1, seg_axis)
    me = lax.axis_index(seg_axis)
    width = partial.shape[1] // segs

    def share(index):
        return lax.dynamic_slice_in_dim(partial, index * width, width, axis=1)

    total = share(me)
    for shift in range(1, segs):
        pairs = [(i, (i + shift) % segs) for i in range(segs)]
        total = total + lax.ppermute(share((me + shift) % segs), seg_axis, pairs)
    return total


def make_shards(chan_axes):
    def shards(spectra, sources):
        whitened = whiten(spectra)
        ch_dev = spectra.shape[2]
        freqs = spectra.shape[3]
        first_row = lax.axis_index(chan_axes) * ch_dev
        lag_table = lag_matrix(freqs, LAGS)
        local_row = sources.reshape(-1) - first_row
        onehot = (local_row[:, None] == jnp.arange(ch_dev, dtype=jnp.int32)[None, :]).astype(
            jnp.bfloat16
        )
        local_spec = jnp.einsum(
            "pc,xscf->xpsf", onehot, whitened, preferred_element_type=jnp.float32
        ).astype(jnp.bfloat16)
        source_spec = gather_sources(local_spec, chan_axes)
        partial = correlate(source_spec, whitened, lag_table, lax.psum(whitened.shape[1], "seg"))
        return sum_over_seg(partial, "seg")

    return shards


def solution(mesh):
    chan = mesh.shape["chan"]
    sizes = tuple(size for _, size in CHAN_FACTORS)
    if math.prod(sizes) == chan:
        devices = mesh.devices.reshape(sizes + (mesh.shape["seg"],))
        fine = Mesh(devices, CHAN_AXES + ("seg",))
        chan_axes = CHAN_AXES
    else:
        fine = mesh
        chan_axes = ("chan",)
    placed = (P(None, "seg", chan_axes, None), P())
    return jax.shard_map(
        make_shards(chan_axes),
        mesh=fine,
        in_specs=placed,
        out_specs=P(None, chan_axes + ("seg",), None),
        check_vma=False,
    )
```

```python
import math

import jax
import jax.numpy as jnp
from jax import lax
from jax.sharding import Mesh, PartitionSpec as P

LAGS = 256
CHAN_FACTORS = (("x", 4), ("zh", 2), ("y", 8), ("c", 2))
CHAN_AXES = tuple(name for name, _ in CHAN_FACTORS)


def whiten(spectra):
    values = spectra.astype(jnp.float32)
    power_mean = jnp.mean(values[0] * values[0] + values[1] * values[1], axis=-1)
    inv_scale = lax.rsqrt(power_mean + 1e-06)
    return (values * inv_scale[None, :, :, None]).astype(jnp.bfloat16)


def lag_matrix(freqs, half_lags):
    period = 2 * freqs
    rows = jnp.arange(freqs, dtype=jnp.int32)
    shifts = jnp.arange(2 * half_lags, dtype=jnp.int32) - half_lags
    phase = jnp.mod(rows[:, None] * shifts[None, :], period)
    angles = phase.astype(jnp.float32) * (2.0 * math.pi / period)
    return jnp.concatenate([jnp.cos(angles), -jnp.sin(angles)], axis=0)


def correlate(source_spec, receiver_spec, lag_table):
    segs = receiver_spec.shape[1]
    freqs = receiver_spec.shape[3]
    a = source_spec[0].astype(jnp.float32)[:, :, None, :]
    b = source_spec[1].astype(jnp.float32)[:, :, None, :]
    c = receiver_spec[0].astype(jnp.float32)[:, None, :, :]
    d = receiver_spec[1].astype(jnp.float32)[:, None, :, :]
    real_part = jnp.sum(a * c + b * d, axis=0)
    imag_part = jnp.sum(a * d - b * c, axis=0)
    stacked = jnp.concatenate([real_part, imag_part], axis=-1) * (1.0 / math.sqrt(segs))
    flat = stacked.reshape(-1, 2 * freqs)
    result = jnp.dot(
        flat, lag_table, precision=lax.Precision.HIGHEST, preferred_element_type=jnp.float32
    ) * (1.0 / math.sqrt(freqs))
    return result.reshape(stacked.shape[0], stacked.shape[1], -1)


def gather_sources(value, chan_axes, seg_axis):
    parts, sources, local_segs, freqs = value.shape
    count = lax.psum(1, chan_axes)
    segs = lax.psum(1, seg_axis)
    chunks = value.reshape(count, -1, freqs)
    rows = chunks.shape[1]
    if chan_axes == CHAN_AXES:
        pair = lax.psum(1, "c")
        rest = ("x", "zh", "y")
        upper = lax.axis_index("c") == 1
        flat = value.reshape(pair, -1, freqs)
        keep = jnp.where(upper, flat[1], flat[0])
        send = jnp.where(upper, flat[0], flat[1])
        half = keep + lax.ppermute(send, "c", [(0, 1), (1, 0)])
        part = half.reshape(count // pair, rows, freqs)
        mine = lax.all_to_all(part, rest, 0, 0).sum(axis=0, dtype=value.dtype)
    else:
        mine = lax.all_to_all(chunks, chan_axes, 0, 0).sum(axis=0, dtype=value.dtype)
    spread = jnp.broadcast_to(mine[None], (count * segs, rows, freqs))
    got = lax.all_to_all(spread, chan_axes + (seg_axis,), 0, 0)
    if chan_axes == CHAN_AXES:
        got = got.reshape(count // pair, pair, segs, rows, freqs).transpose(1, 0, 2, 3, 4)
    split = local_segs // rows
    got = got.reshape(parts, sources, split, segs, rows, freqs).transpose(0, 3, 2, 4, 1, 5)
    return got.reshape(parts, segs * local_segs, sources, freqs)


def regroup_receivers(whitened, seg_axis):
    segs = lax.psum(1, seg_axis)
    me = lax.axis_index(seg_axis)
    parts, local_segs, ch_dev, freqs = whitened.shape
    groups = whitened.reshape(parts, local_segs, segs, ch_dev // segs, freqs)

    def group(index):
        return lax.dynamic_index_in_dim(groups, index, axis=2, keepdims=False)

    blocks = [group(me)]
    for shift in range(1, segs):
        pairs = [(i, (i + shift) % segs) for i in range(segs)]
        blocks.append(lax.ppermute(group((me + shift) % segs), seg_axis, pairs))
    return jnp.concatenate(blocks[::-1], axis=1)


def rotate_segments(source_spec, seg_axis):
    segs = lax.psum(1, seg_axis)
    me = lax.axis_index(seg_axis)
    parts, all_segs, sources, freqs = source_spec.shape
    doubled = jnp.concatenate([source_spec, source_spec], axis=1)
    return lax.dynamic_slice_in_dim(doubled, ((me + 1) % segs) * (all_segs // segs), all_segs, axis=1)


def make_shards(chan_axes):
    def shards(spectra, sources):
        whitened = whiten(spectra)
        regrouped = regroup_receivers(whitened, "seg")
        ch_dev = spectra.shape[2]
        freqs = spectra.shape[3]
        first_row = lax.axis_index(chan_axes) * ch_dev
        lag_table = lag_matrix(freqs, LAGS)
        local_row = sources.reshape(-1) - first_row
        onehot = (local_row[:, None] == jnp.arange(ch_dev, dtype=jnp.int32)[None, :]).astype(
            jnp.bfloat16
        )
        local_spec = jnp.einsum(
            "pc,xscf->xpsf", onehot, whitened, preferred_element_type=jnp.float32
        ).astype(jnp.bfloat16)
        regrouped, local_spec = lax.optimization_barrier((regrouped, local_spec))
        source_spec = rotate_segments(gather_sources(local_spec, chan_axes, "seg"), "seg")
        return correlate(source_spec, regrouped, lag_table)

    return shards


def solution(mesh):
    chan = mesh.shape["chan"]
    sizes = tuple(size for _, size in CHAN_FACTORS)
    if math.prod(sizes) == chan:
        devices = mesh.devices.reshape(sizes + (mesh.shape["seg"],))
        fine = Mesh(devices, CHAN_AXES + ("seg",))
        chan_axes = CHAN_AXES
    else:
        fine = mesh
        chan_axes = ("chan",)
    placed = (P(None, "seg", chan_axes, None), P())
    return jax.shard_map(
        make_shards(chan_axes),
        mesh=fine,
        in_specs=placed,
        out_specs=P(None, chan_axes + ("seg",), None),
        check_vma=False,
    )
```

```python
import math

import jax
import jax.numpy as jnp
from jax import lax
from jax.sharding import Mesh, PartitionSpec as P

LAGS = 256
CHAN_FACTORS = (("x", 4), ("zh", 2), ("y", 8), ("c", 2))
CHAN_AXES = tuple(name for name, _ in CHAN_FACTORS)


def whiten(spectra):
    values = spectra.astype(jnp.float32)
    power_mean = jnp.mean(values[0] * values[0] + values[1] * values[1], axis=-1)
    inv_scale = lax.rsqrt(power_mean + 1e-06)
    return (values * inv_scale[None, :, :, None]).astype(jnp.bfloat16)


def lag_matrix(freqs, half_lags):
    period = 2 * freqs
    rows = jnp.arange(freqs, dtype=jnp.int32)
    shifts = jnp.arange(2 * half_lags, dtype=jnp.int32) - half_lags
    phase = jnp.mod(rows[:, None] * shifts[None, :], period)
    angles = phase.astype(jnp.float32) * (2.0 * math.pi / period)
    return jnp.concatenate([jnp.cos(angles), -jnp.sin(angles)], axis=0)


def correlate(source_spec, receiver_spec, lag_table):
    segs = receiver_spec.shape[1]
    freqs = receiver_spec.shape[3]
    a = source_spec[0].astype(jnp.float32)[:, :, None, :]
    b = source_spec[1].astype(jnp.float32)[:, :, None, :]
    c = receiver_spec[0].astype(jnp.float32)[:, None, :, :]
    d = receiver_spec[1].astype(jnp.float32)[:, None, :, :]
    real_part = jnp.sum(a * c + b * d, axis=0)
    imag_part = jnp.sum(a * d - b * c, axis=0)
    stacked = jnp.concatenate([real_part, imag_part], axis=-1) * (1.0 / math.sqrt(segs))
    flat = stacked.reshape(-1, 2 * freqs)
    result = jnp.dot(
        flat, lag_table, precision=lax.Precision.HIGHEST, preferred_element_type=jnp.float32
    ) * (1.0 / math.sqrt(freqs))
    return result.reshape(stacked.shape[0], stacked.shape[1], -1)


def gather_sources(value, chan_axes, seg_axis):
    parts, sources, local_segs, freqs = value.shape
    count = lax.psum(1, chan_axes)
    segs = lax.psum(1, seg_axis)
    chunks = value.reshape(count, -1, freqs)
    rows = chunks.shape[1]
    if chan_axes == CHAN_AXES:
        pair = lax.psum(1, "c")
        rest = ("x", "zh", "y")
        upper = lax.axis_index("c") == 1
        flat = value.reshape(pair, -1, freqs)
        keep = jnp.where(upper, flat[1], flat[0])
        send = jnp.where(upper, flat[0], flat[1])
        half = keep + lax.ppermute(send, "c", [(0, 1), (1, 0)])
        part = half.reshape(count // pair, rows, freqs)
        mine = lax.all_to_all(part, rest, 0, 0).sum(axis=0, dtype=value.dtype)
    else:
        mine = lax.all_to_all(chunks, chan_axes, 0, 0).sum(axis=0, dtype=value.dtype)
    if chan_axes == CHAN_AXES:
        far = lax.axis_index("zh") == 1
        other = lax.ppermute(mine, "zh", [(0, 1), (1, 0)])
        both = jnp.stack([jnp.where(far, other, mine), jnp.where(far, mine, other)])
        near = ("x", "y", "c", seg_axis)
        spread = jnp.broadcast_to(both[None], (count * segs // 2,) + both.shape)
        got = lax.all_to_all(spread, near, 0, 0)
        got = got.reshape(4, 8, pair, segs, 2, rows, freqs).transpose(2, 0, 4, 1, 3, 5, 6)
    else:
        spread = jnp.broadcast_to(mine[None], (count * segs, rows, freqs))
        got = lax.all_to_all(spread, chan_axes + (seg_axis,), 0, 0)
    split = local_segs // rows
    got = got.reshape(parts, sources, split, segs, rows, freqs).transpose(0, 3, 2, 4, 1, 5)
    return got.reshape(parts, segs * local_segs, sources, freqs)


def regroup_receivers(whitened, seg_axis):
    segs = lax.psum(1, seg_axis)
    me = lax.axis_index(seg_axis)
    parts, local_segs, ch_dev, freqs = whitened.shape
    groups = whitened.reshape(parts, local_segs, segs, ch_dev // segs, freqs)

    def group(index):
        return lax.dynamic_index_in_dim(groups, index, axis=2, keepdims=False)

    blocks = [group(me)]
    for shift in range(1, segs):
        pairs = [(i, (i + shift) % segs) for i in range(segs)]
        blocks.append(lax.ppermute(group((me + shift) % segs), seg_axis, pairs))
    return jnp.concatenate(blocks[::-1], axis=1)


def rotate_segments(source_spec, seg_axis):
    segs = lax.psum(1, seg_axis)
    me = lax.axis_index(seg_axis)
    parts, all_segs, sources, freqs = source_spec.shape
    doubled = jnp.concatenate([source_spec, source_spec], axis=1)
    return lax.dynamic_slice_in_dim(doubled, ((me + 1) % segs) * (all_segs // segs), all_segs, axis=1)


def make_shards(chan_axes):
    def shards(spectra, sources):
        whitened = whiten(spectra)
        regrouped = regroup_receivers(whitened, "seg")
        ch_dev = spectra.shape[2]
        freqs = spectra.shape[3]
        first_row = lax.axis_index(chan_axes) * ch_dev
        lag_table = lag_matrix(freqs, LAGS)
        local_row = sources.reshape(-1) - first_row
        onehot = (local_row[:, None] == jnp.arange(ch_dev, dtype=jnp.int32)[None, :]).astype(
            jnp.bfloat16
        )
        local_spec = jnp.einsum(
            "pc,xscf->xpsf", onehot, whitened, preferred_element_type=jnp.float32
        ).astype(jnp.bfloat16)
        source_spec = rotate_segments(gather_sources(local_spec, chan_axes, "seg"), "seg")
        return correlate(source_spec, regrouped, lag_table)

    return shards


def solution(mesh):
    chan = mesh.shape["chan"]
    sizes = tuple(size for _, size in CHAN_FACTORS)
    if math.prod(sizes) == chan:
        devices = mesh.devices.reshape(sizes + (mesh.shape["seg"],))
        fine = Mesh(devices, CHAN_AXES + ("seg",))
        chan_axes = CHAN_AXES
    else:
        fine = mesh
        chan_axes = ("chan",)
    placed = (P(None, "seg", chan_axes, None), P())
    return jax.shard_map(
        make_shards(chan_axes),
        mesh=fine,
        in_specs=placed,
        out_specs=P(None, chan_axes + ("seg",), None),
        check_vma=False,
    )
```

```python
import math

import jax
import jax.numpy as jnp
from jax import lax
from jax.sharding import Mesh, PartitionSpec as P

LAGS = 256
CHAN_FACTORS = (("x", 4), ("zh", 2), ("y", 8), ("c", 2))
CHAN_AXES = tuple(name for name, _ in CHAN_FACTORS)


def whiten(spectra):
    values = spectra.astype(jnp.float32)
    power_mean = jnp.mean(values[0] * values[0] + values[1] * values[1], axis=-1)
    inv_scale = lax.rsqrt(power_mean + 1e-06)
    return (values * inv_scale[None, :, :, None]).astype(jnp.bfloat16)


def lag_matrix(freqs, half_lags):
    period = 2 * freqs
    rows = jnp.arange(freqs, dtype=jnp.int32)
    shifts = jnp.arange(2 * half_lags, dtype=jnp.int32) - half_lags
    phase = jnp.mod(rows[:, None] * shifts[None, :], period)
    angles = phase.astype(jnp.float32) * (2.0 * math.pi / period)
    return jnp.concatenate([jnp.cos(angles), -jnp.sin(angles)], axis=0)


def correlate(source_spec, receiver_spec, lag_table):
    segs = receiver_spec.shape[1]
    freqs = receiver_spec.shape[3]
    a = source_spec[0].astype(jnp.float32)[:, :, None, :]
    b = source_spec[1].astype(jnp.float32)[:, :, None, :]
    c = receiver_spec[0].astype(jnp.float32)[:, None, :, :]
    d = receiver_spec[1].astype(jnp.float32)[:, None, :, :]
    real_part = jnp.sum(a * c + b * d, axis=0)
    imag_part = jnp.sum(a * d - b * c, axis=0)
    stacked = jnp.concatenate([real_part, imag_part], axis=-1) * (1.0 / math.sqrt(segs))
    flat = stacked.reshape(-1, 2 * freqs)
    result = jnp.dot(
        flat, lag_table, precision=lax.Precision.HIGHEST, preferred_element_type=jnp.float32
    ) * (1.0 / math.sqrt(freqs))
    return result.reshape(stacked.shape[0], stacked.shape[1], -1)


def gather_sources(value, chan_axes, seg_axis):
    parts, sources, local_segs, freqs = value.shape
    count = lax.psum(1, chan_axes)
    segs = lax.psum(1, seg_axis)
    chunks = value.reshape(count, -1, freqs)
    rows = chunks.shape[1]
    if chan_axes == CHAN_AXES:
        pair = lax.psum(1, "c")
        rest = ("x", "zh", "y")
        upper = lax.axis_index("c") == 1
        flat = value.reshape(pair, -1, freqs)
        keep = jnp.where(upper, flat[1], flat[0])
        send = jnp.where(upper, flat[0], flat[1])
        half = keep + lax.ppermute(send, "c", [(0, 1), (1, 0)])
        part = half.reshape(count // pair, rows, freqs)
        mine = lax.all_to_all(part, rest, 0, 0).sum(axis=0, dtype=value.dtype)
    else:
        mine = lax.all_to_all(chunks, chan_axes, 0, 0).sum(axis=0, dtype=value.dtype)
    if chan_axes == CHAN_AXES:
        spread = jnp.broadcast_to(mine[None], (count * segs // pair, rows, freqs))
        half_got = lax.all_to_all(spread, rest + (seg_axis,), 0, 0)
        sibling = lax.ppermute(half_got, "c", [(0, 1), (1, 0)])
        got = jnp.stack([jnp.where(upper, sibling, half_got), jnp.where(upper, half_got, sibling)])
    else:
        spread = jnp.broadcast_to(mine[None], (count * segs, rows, freqs))
        got = lax.all_to_all(spread, chan_axes + (seg_axis,), 0, 0)
    split = local_segs // rows
    got = got.reshape(parts, sources, split, segs, rows, freqs).transpose(0, 3, 2, 4, 1, 5)
    return got.reshape(parts, segs * local_segs, sources, freqs)


def regroup_receivers(whitened, seg_axis):
    segs = lax.psum(1, seg_axis)
    me = lax.axis_index(seg_axis)
    parts, local_segs, ch_dev, freqs = whitened.shape
    groups = whitened.reshape(parts, local_segs, segs, ch_dev // segs, freqs)

    def group(index):
        return lax.dynamic_index_in_dim(groups, index, axis=2, keepdims=False)

    blocks = [group(me)]
    for shift in range(1, segs):
        pairs = [(i, (i + shift) % segs) for i in range(segs)]
        blocks.append(lax.ppermute(group((me + shift) % segs), seg_axis, pairs))
    return jnp.concatenate(blocks[::-1], axis=1)


def rotate_segments(source_spec, seg_axis):
    segs = lax.psum(1, seg_axis)
    me = lax.axis_index(seg_axis)
    parts, all_segs, sources, freqs = source_spec.shape
    doubled = jnp.concatenate([source_spec, source_spec], axis=1)
    return lax.dynamic_slice_in_dim(doubled, ((me + 1) % segs) * (all_segs // segs), all_segs, axis=1)


def make_shards(chan_axes):
    def shards(spectra, sources):
        whitened = whiten(spectra)
        regrouped = regroup_receivers(whitened, "seg")
        ch_dev = spectra.shape[2]
        freqs = spectra.shape[3]
        first_row = lax.axis_index(chan_axes) * ch_dev
        lag_table = lag_matrix(freqs, LAGS)
        local_row = sources.reshape(-1) - first_row
        onehot = (local_row[:, None] == jnp.arange(ch_dev, dtype=jnp.int32)[None, :]).astype(
            jnp.bfloat16
        )
        local_spec = jnp.einsum(
            "pc,xscf->xpsf", onehot, whitened, preferred_element_type=jnp.float32
        ).astype(jnp.bfloat16)
        source_spec = rotate_segments(gather_sources(local_spec, chan_axes, "seg"), "seg")
        return correlate(source_spec, regrouped, lag_table)

    return shards


def solution(mesh):
    chan = mesh.shape["chan"]
    sizes = tuple(size for _, size in CHAN_FACTORS)
    if math.prod(sizes) == chan:
        devices = mesh.devices.reshape(sizes + (mesh.shape["seg"],))
        fine = Mesh(devices, CHAN_AXES + ("seg",))
        chan_axes = CHAN_AXES
    else:
        fine = mesh
        chan_axes = ("chan",)
    placed = (P(None, "seg", chan_axes, None), P())
    return jax.shard_map(
        make_shards(chan_axes),
        mesh=fine,
        in_specs=placed,
        out_specs=P(None, chan_axes + ("seg",), None),
        check_vma=False,
    )
```

```python
import math

import jax
import jax.numpy as jnp
from jax import lax
from jax.sharding import Mesh, PartitionSpec as P

LAGS = 256
CHAN_FACTORS = (("x", 4), ("zh", 2), ("y", 8), ("c", 2))
CHAN_AXES = tuple(name for name, _ in CHAN_FACTORS)


def whiten(spectra):
    values = spectra.astype(jnp.float32)
    power_mean = jnp.mean(values[0] * values[0] + values[1] * values[1], axis=-1)
    inv_scale = lax.rsqrt(power_mean + 1e-06)
    return (values * inv_scale[None, :, :, None]).astype(jnp.bfloat16)


def lag_matrix(freqs, half_lags):
    period = 2 * freqs
    rows = jnp.arange(freqs, dtype=jnp.int32)
    shifts = jnp.arange(2 * half_lags, dtype=jnp.int32) - half_lags
    phase = jnp.mod(rows[:, None] * shifts[None, :], period)
    angles = phase.astype(jnp.float32) * (2.0 * math.pi / period)
    return jnp.concatenate([jnp.cos(angles), -jnp.sin(angles)], axis=0)


def correlate(source_spec, receiver_spec, lag_table):
    segs = receiver_spec.shape[1]
    freqs = receiver_spec.shape[3]
    a = source_spec[0].astype(jnp.float32)[:, :, None, :]
    b = source_spec[1].astype(jnp.float32)[:, :, None, :]
    c = receiver_spec[0].astype(jnp.float32)[:, None, :, :]
    d = receiver_spec[1].astype(jnp.float32)[:, None, :, :]
    real_part = jnp.sum(a * c + b * d, axis=0)
    imag_part = jnp.sum(a * d - b * c, axis=0)
    stacked = jnp.concatenate([real_part, imag_part], axis=-1) * (1.0 / math.sqrt(segs))
    flat = stacked.reshape(-1, 2 * freqs)
    result = jnp.dot(
        flat, lag_table, precision=lax.Precision.HIGHEST, preferred_element_type=jnp.float32
    ) * (1.0 / math.sqrt(freqs))
    return result.reshape(stacked.shape[0], stacked.shape[1], -1)


def gather_sources(value, chan_axes, seg_axis, companion):
    parts, sources, local_segs, freqs = value.shape
    count = lax.psum(1, chan_axes)
    segs = lax.psum(1, seg_axis)
    chunks = value.reshape(count, -1, freqs)
    rows = chunks.shape[1]
    if chan_axes == CHAN_AXES:
        pair = lax.psum(1, "c")
        rest = ("x", "zh", "y")
        upper = lax.axis_index("c") == 1
        flat = value.reshape(pair, -1, freqs)
        keep = jnp.where(upper, flat[1], flat[0])
        send = jnp.where(upper, flat[0], flat[1])
        half = keep + lax.ppermute(send, "c", [(0, 1), (1, 0)])
        part = half.reshape(count // pair, rows, freqs)
        mine = lax.all_to_all(part, rest, 0, 0).sum(axis=0, dtype=value.dtype)
        mine, companion = lax.optimization_barrier((mine, companion))
    else:
        mine = lax.all_to_all(chunks, chan_axes, 0, 0).sum(axis=0, dtype=value.dtype)
    if chan_axes == CHAN_AXES:
        spread = jnp.broadcast_to(mine[None], (count * segs // pair, rows, freqs))
        half_got = lax.all_to_all(spread, rest + (seg_axis,), 0, 0)
        sibling = lax.ppermute(half_got, "c", [(0, 1), (1, 0)])
        got = jnp.stack([jnp.where(upper, sibling, half_got), jnp.where(upper, half_got, sibling)])
    else:
        spread = jnp.broadcast_to(mine[None], (count * segs, rows, freqs))
        got = lax.all_to_all(spread, chan_axes + (seg_axis,), 0, 0)
    split = local_segs // rows
    got = got.reshape(parts, sources, split, segs, rows, freqs).transpose(0, 3, 2, 4, 1, 5)
    return got.reshape(parts, segs * local_segs, sources, freqs), companion


def regroup_receivers(whitened, seg_axis):
    segs = lax.psum(1, seg_axis)
    me = lax.axis_index(seg_axis)
    parts, local_segs, ch_dev, freqs = whitened.shape
    groups = whitened.reshape(parts, local_segs, segs, ch_dev // segs, freqs)

    def group(index):
        return lax.dynamic_index_in_dim(groups, index, axis=2, keepdims=False)

    blocks = [group(me)]
    for shift in range(1, segs):
        pairs = [(i, (i + shift) % segs) for i in range(segs)]
        blocks.append(lax.ppermute(group((me + shift) % segs), seg_axis, pairs))
    return jnp.concatenate(blocks[::-1], axis=1)


def rotate_segments(source_spec, seg_axis):
    segs = lax.psum(1, seg_axis)
    me = lax.axis_index(seg_axis)
    parts, all_segs, sources, freqs = source_spec.shape
    doubled = jnp.concatenate([source_spec, source_spec], axis=1)
    return lax.dynamic_slice_in_dim(doubled, ((me + 1) % segs) * (all_segs // segs), all_segs, axis=1)


def make_shards(chan_axes):
    def shards(spectra, sources):
        whitened = whiten(spectra)
        regrouped = regroup_receivers(whitened, "seg")
        ch_dev = spectra.shape[2]
        freqs = spectra.shape[3]
        first_row = lax.axis_index(chan_axes) * ch_dev
        lag_table = lag_matrix(freqs, LAGS)
        local_row = sources.reshape(-1) - first_row
        onehot = (local_row[:, None] == jnp.arange(ch_dev, dtype=jnp.int32)[None, :]).astype(
            jnp.bfloat16
        )
        local_spec = jnp.einsum(
            "pc,xscf->xpsf", onehot, whitened, preferred_element_type=jnp.float32
        ).astype(jnp.bfloat16)
        source_spec, regrouped = gather_sources(local_spec, chan_axes, "seg", regrouped)
        source_spec = rotate_segments(source_spec, "seg")
        return correlate(source_spec, regrouped, lag_table)

    return shards


def solution(mesh):
    chan = mesh.shape["chan"]
    sizes = tuple(size for _, size in CHAN_FACTORS)
    if math.prod(sizes) == chan:
        devices = mesh.devices.reshape(sizes + (mesh.shape["seg"],))
        fine = Mesh(devices, CHAN_AXES + ("seg",))
        chan_axes = CHAN_AXES
    else:
        fine = mesh
        chan_axes = ("chan",)
    placed = (P(None, "seg", chan_axes, None), P())
    return jax.shard_map(
        make_shards(chan_axes),
        mesh=fine,
        in_specs=placed,
        out_specs=P(None, chan_axes + ("seg",), None),
        check_vma=False,
    )
```

```python
import math

import jax
import jax.numpy as jnp
from jax import lax
from jax.sharding import Mesh, PartitionSpec as P

LAGS = 256
CHAN_FACTORS = (("x", 4), ("zh", 2), ("y", 8), ("c", 2))
CHAN_AXES = tuple(name for name, _ in CHAN_FACTORS)


def whiten(spectra):
    values = spectra.astype(jnp.float32)
    power_mean = jnp.mean(values[0] * values[0] + values[1] * values[1], axis=-1)
    inv_scale = lax.rsqrt(power_mean + 1e-06)
    return (values * inv_scale[None, :, :, None]).astype(jnp.bfloat16)


def lag_matrix(freqs, half_lags):
    period = 2 * freqs
    rows = jnp.arange(freqs, dtype=jnp.int32)
    shifts = jnp.arange(2 * half_lags, dtype=jnp.int32) - half_lags
    phase = jnp.mod(rows[:, None] * shifts[None, :], period)
    angles = phase.astype(jnp.float32) * (2.0 * math.pi / period)
    return jnp.concatenate([jnp.cos(angles), -jnp.sin(angles)], axis=0)


def correlate(source_spec, receiver_spec, lag_table):
    segs = receiver_spec.shape[1]
    freqs = receiver_spec.shape[3]
    a = source_spec[0].astype(jnp.float32)[:, :, None, :]
    b = source_spec[1].astype(jnp.float32)[:, :, None, :]
    c = receiver_spec[0].astype(jnp.float32)[:, None, :, :]
    d = receiver_spec[1].astype(jnp.float32)[:, None, :, :]
    real_part = jnp.sum(a * c + b * d, axis=0)
    imag_part = jnp.sum(a * d - b * c, axis=0)
    stacked = jnp.concatenate([real_part, imag_part], axis=-1) * (1.0 / math.sqrt(segs))
    flat = stacked.reshape(-1, 2 * freqs)
    result = jnp.dot(
        flat, lag_table, precision=lax.Precision.HIGHEST, preferred_element_type=jnp.float32
    ) * (1.0 / math.sqrt(freqs))
    return result.reshape(stacked.shape[0], stacked.shape[1], -1)


def gather_sources(value, chan_axes, seg_axis, companion):
    parts, sources, local_segs, freqs = value.shape
    count = lax.psum(1, chan_axes)
    segs = lax.psum(1, seg_axis)
    chunks = value.reshape(count, -1, freqs)
    rows = chunks.shape[1]
    if chan_axes == CHAN_AXES:
        pair = lax.psum(1, "c")
        rest = ("x", "zh", "y")
        upper = lax.axis_index("c") == 1
        flat = value.reshape(pair, -1, freqs)
        keep = jnp.where(upper, flat[1], flat[0])
        send = jnp.where(upper, flat[0], flat[1])
        half = keep + lax.ppermute(send, "c", [(0, 1), (1, 0)])
        part = half.reshape(count // pair, rows, freqs)
        mine = lax.all_to_all(part, rest, 0, 0).sum(axis=0, dtype=value.dtype)
        mine, companion = lax.optimization_barrier((mine, companion))
    else:
        mine = lax.all_to_all(chunks, chan_axes, 0, 0).sum(axis=0, dtype=value.dtype)
    if chan_axes == CHAN_AXES:
        spread = jnp.broadcast_to(mine[None], (count * segs // pair, rows, freqs))
        half_got = lax.all_to_all(spread, rest + (seg_axis,), 0, 0)
        sibling = lax.ppermute(half_got, "c", [(0, 1), (1, 0)])
        got = jnp.stack([jnp.where(upper, sibling, half_got), jnp.where(upper, half_got, sibling)])
    else:
        spread = jnp.broadcast_to(mine[None], (count * segs, rows, freqs))
        got = lax.all_to_all(spread, chan_axes + (seg_axis,), 0, 0)
    split = local_segs // rows
    got = got.reshape(parts, sources, split, segs, rows, freqs).transpose(0, 3, 2, 4, 1, 5)
    return got.reshape(parts, segs * local_segs, sources, freqs), companion


def regroup_receivers(whitened, seg_axis):
    segs = lax.psum(1, seg_axis)
    me = lax.axis_index(seg_axis)
    parts, local_segs, ch_dev, freqs = whitened.shape
    groups = whitened.reshape(parts, local_segs, segs, ch_dev // segs, freqs)

    def group(index):
        return lax.dynamic_index_in_dim(groups, index, axis=2, keepdims=False)

    blocks = [group(me)]
    for shift in range(1, segs):
        pairs = [(i, (i + shift) % segs) for i in range(segs)]
        blocks.append(lax.ppermute(group((me + shift) % segs), seg_axis, pairs))
    return jnp.concatenate(blocks[::-1], axis=1)


def rotate_segments(source_spec, seg_axis):
    segs = lax.psum(1, seg_axis)
    me = lax.axis_index(seg_axis)
    parts, all_segs, sources, freqs = source_spec.shape
    doubled = jnp.concatenate([source_spec, source_spec], axis=1)
    return lax.dynamic_slice_in_dim(doubled, ((me + 1) % segs) * (all_segs // segs), all_segs, axis=1)


def make_shards(chan_axes):
    def shards(spectra, sources):
        whitened = whiten(spectra)
        regrouped = regroup_receivers(whitened, "seg")
        ch_dev = spectra.shape[2]
        freqs = spectra.shape[3]
        first_row = lax.axis_index(chan_axes) * ch_dev
        lag_table = lag_matrix(freqs, LAGS)
        local_row = sources.reshape(-1) - first_row
        onehot = (local_row[:, None] == jnp.arange(ch_dev, dtype=jnp.int32)[None, :]).astype(
            jnp.bfloat16
        )
        local_spec = jnp.einsum(
            "pc,xscf->xpsf", onehot, whitened, preferred_element_type=jnp.float32
        ).astype(jnp.bfloat16)
        source_spec, (regrouped, lag_table) = gather_sources(
            local_spec, chan_axes, "seg", (regrouped, lag_table)
        )
        source_spec = rotate_segments(source_spec, "seg")
        return correlate(source_spec, regrouped, lag_table)

    return shards


def solution(mesh):
    chan = mesh.shape["chan"]
    sizes = tuple(size for _, size in CHAN_FACTORS)
    if math.prod(sizes) == chan:
        devices = mesh.devices.reshape(sizes + (mesh.shape["seg"],))
        fine = Mesh(devices, CHAN_AXES + ("seg",))
        chan_axes = CHAN_AXES
    else:
        fine = mesh
        chan_axes = ("chan",)
    placed = (P(None, "seg", chan_axes, None), P())
    return jax.shard_map(
        make_shards(chan_axes),
        mesh=fine,
        in_specs=placed,
        out_specs=P(None, chan_axes + ("seg",), None),
        check_vma=False,
    )
```

```python
import math

import jax
import jax.numpy as jnp
from jax import lax
from jax.sharding import Mesh, PartitionSpec as P

LAGS = 256
CHAN_FACTORS = (("x", 4), ("zh", 2), ("y", 8), ("c", 2))
CHAN_AXES = tuple(name for name, _ in CHAN_FACTORS)


def whiten(spectra):
    values = spectra.astype(jnp.float32)
    power_mean = jnp.mean(values[0] * values[0] + values[1] * values[1], axis=-1)
    inv_scale = lax.rsqrt(power_mean + 1e-06)
    return (values * inv_scale[None, :, :, None]).astype(jnp.bfloat16)


def lag_matrix(freqs, half_lags):
    period = 2 * freqs
    rows = jnp.arange(freqs, dtype=jnp.int32)
    shifts = jnp.arange(2 * half_lags, dtype=jnp.int32) - half_lags
    phase = jnp.mod(rows[:, None] * shifts[None, :], period)
    angles = phase.astype(jnp.float32) * (2.0 * math.pi / period)
    return jnp.concatenate([jnp.cos(angles), -jnp.sin(angles)], axis=0)


def correlate(source_spec, receiver_spec, lag_table):
    segs = receiver_spec.shape[1]
    freqs = receiver_spec.shape[3]
    a = source_spec[0].astype(jnp.float32)[:, :, None, :]
    b = source_spec[1].astype(jnp.float32)[:, :, None, :]
    c = receiver_spec[0].astype(jnp.float32)[:, None, :, :]
    d = receiver_spec[1].astype(jnp.float32)[:, None, :, :]
    real_part = jnp.sum(a * c + b * d, axis=0)
    imag_part = jnp.sum(a * d - b * c, axis=0)
    stacked = jnp.concatenate([real_part, imag_part], axis=-1) * (1.0 / math.sqrt(segs))
    flat = stacked.reshape(-1, 2 * freqs)
    result = jnp.dot(
        flat, lag_table, precision=lax.Precision.HIGHEST, preferred_element_type=jnp.float32
    ) * (1.0 / math.sqrt(freqs))
    return result.reshape(stacked.shape[0], stacked.shape[1], -1)


def gather_sources(value, chan_axes, seg_axis, companion):
    parts, sources, local_segs, freqs = value.shape
    count = lax.psum(1, chan_axes)
    segs = lax.psum(1, seg_axis)
    chunks = value.reshape(count, -1, freqs)
    rows = chunks.shape[1]
    if chan_axes == CHAN_AXES:
        pair = lax.psum(1, "c")
        rest = ("x", "zh", "y")
        upper = lax.axis_index("c") == 1
        flat = value.reshape(pair, -1, freqs)
        keep = jnp.where(upper, flat[1], flat[0])
        send = jnp.where(upper, flat[0], flat[1])
        half = keep + lax.ppermute(send, "c", [(0, 1), (1, 0)])
        part = half.reshape(count // pair, rows, freqs)
        mine = lax.all_to_all(part, rest, 0, 0).sum(axis=0, dtype=value.dtype)
        mine, companion = lax.optimization_barrier((mine, companion))
    else:
        mine = lax.all_to_all(chunks, chan_axes, 0, 0).sum(axis=0, dtype=value.dtype)
    if chan_axes == CHAN_AXES:
        me = lax.axis_index(seg_axis)
        came = [mine]
        for shift in range(1, segs):
            pairs = [(i, (i + shift) % segs) for i in range(segs)]
            came.append(lax.ppermute(mine, seg_axis, pairs))
        ring = jnp.stack(came[::-1] * 2)
        start = (segs - (me + 1) % segs) % segs
        ordered = lax.dynamic_slice_in_dim(ring, start, segs, axis=0)
        spread = jnp.broadcast_to(ordered[None], (count // pair,) + ordered.shape)
        half_got = lax.all_to_all(spread, rest, 0, 0).reshape(count * segs // pair, rows, freqs)
        sibling = lax.ppermute(half_got, "c", [(0, 1), (1, 0)])
        got = jnp.stack([jnp.where(upper, sibling, half_got), jnp.where(upper, half_got, sibling)])
    else:
        spread = jnp.broadcast_to(mine[None], (count * segs, rows, freqs))
        got = lax.all_to_all(spread, chan_axes + (seg_axis,), 0, 0)
    split = local_segs // rows
    got = got.reshape(parts, sources, split, segs, rows, freqs).transpose(0, 3, 2, 4, 1, 5)
    return got.reshape(parts, segs * local_segs, sources, freqs), companion


def regroup_receivers(whitened, seg_axis):
    segs = lax.psum(1, seg_axis)
    me = lax.axis_index(seg_axis)
    parts, local_segs, ch_dev, freqs = whitened.shape
    groups = whitened.reshape(parts, local_segs, segs, ch_dev // segs, freqs)

    def group(index):
        return lax.dynamic_index_in_dim(groups, index, axis=2, keepdims=False)

    blocks = [group(me)]
    for shift in range(1, segs):
        pairs = [(i, (i + shift) % segs) for i in range(segs)]
        blocks.append(lax.ppermute(group((me + shift) % segs), seg_axis, pairs))
    return jnp.concatenate(blocks[::-1], axis=1)


def rotate_segments(source_spec, seg_axis):
    segs = lax.psum(1, seg_axis)
    me = lax.axis_index(seg_axis)
    parts, all_segs, sources, freqs = source_spec.shape
    doubled = jnp.concatenate([source_spec, source_spec], axis=1)
    return lax.dynamic_slice_in_dim(doubled, ((me + 1) % segs) * (all_segs // segs), all_segs, axis=1)


def make_shards(chan_axes):
    def shards(spectra, sources):
        whitened = whiten(spectra)
        regrouped = regroup_receivers(whitened, "seg")
        ch_dev = spectra.shape[2]
        freqs = spectra.shape[3]
        first_row = lax.axis_index(chan_axes) * ch_dev
        lag_table = lag_matrix(freqs, LAGS)
        local_row = sources.reshape(-1) - first_row
        onehot = (local_row[:, None] == jnp.arange(ch_dev, dtype=jnp.int32)[None, :]).astype(
            jnp.bfloat16
        )
        local_spec = jnp.einsum(
            "pc,xscf->xpsf", onehot, whitened, preferred_element_type=jnp.float32
        ).astype(jnp.bfloat16)
        source_spec, (regrouped, lag_table) = gather_sources(
            local_spec, chan_axes, "seg", (regrouped, lag_table)
        )
        source_spec = rotate_segments(source_spec, "seg")
        return correlate(source_spec, regrouped, lag_table)

    return shards


def solution(mesh):
    chan = mesh.shape["chan"]
    sizes = tuple(size for _, size in CHAN_FACTORS)
    if math.prod(sizes) == chan:
        devices = mesh.devices.reshape(sizes + (mesh.shape["seg"],))
        fine = Mesh(devices, CHAN_AXES + ("seg",))
        chan_axes = CHAN_AXES
    else:
        fine = mesh
        chan_axes = ("chan",)
    placed = (P(None, "seg", chan_axes, None), P())
    return jax.shard_map(
        make_shards(chan_axes),
        mesh=fine,
        in_specs=placed,
        out_specs=P(None, chan_axes + ("seg",), None),
        check_vma=False,
    )
```

```python
import math

import jax
import jax.numpy as jnp
from jax import lax
from jax.sharding import Mesh, PartitionSpec as P

LAGS = 256
CHAN_FACTORS = (("x", 4), ("zh", 2), ("y", 8), ("c", 2))
CHAN_AXES = tuple(name for name, _ in CHAN_FACTORS)


def whiten(spectra):
    values = spectra.astype(jnp.float32)
    power_mean = jnp.mean(values[0] * values[0] + values[1] * values[1], axis=-1)
    inv_scale = lax.rsqrt(power_mean + 1e-06)
    return (values * inv_scale[None, :, :, None]).astype(jnp.bfloat16)


def lag_matrix(freqs, half_lags):
    period = 2 * freqs
    rows = jnp.arange(freqs, dtype=jnp.int32)
    shifts = jnp.arange(2 * half_lags, dtype=jnp.int32) - half_lags
    phase = jnp.mod(rows[:, None] * shifts[None, :], period)
    angles = phase.astype(jnp.float32) * (2.0 * math.pi / period)
    return jnp.concatenate([jnp.cos(angles), -jnp.sin(angles)], axis=0)


def correlate(source_spec, receiver_spec, lag_table, swapped):
    segs = receiver_spec.shape[1]
    freqs = receiver_spec.shape[3]
    a = source_spec[0].astype(jnp.float32)[:, :, None, :]
    b = source_spec[1].astype(jnp.float32)[:, :, None, :]
    first = jnp.where(swapped, receiver_spec[1], receiver_spec[0])
    second = jnp.where(swapped, receiver_spec[0], receiver_spec[1])
    c = first.astype(jnp.float32)[:, None, :, :]
    d = second.astype(jnp.float32)[:, None, :, :]
    sign = jnp.where(swapped, -1.0, 1.0).astype(jnp.float32)
    real_part = jnp.sum(a * c + b * d, axis=0)
    imag_part = jnp.sum(a * d - b * c, axis=0) * sign
    stacked = jnp.concatenate([real_part, imag_part], axis=-1) * (1.0 / math.sqrt(segs))
    flat = stacked.reshape(-1, 2 * freqs)
    result = jnp.dot(
        flat, lag_table, precision=lax.Precision.HIGHEST, preferred_element_type=jnp.float32
    ) * (1.0 / math.sqrt(freqs))
    return result.reshape(stacked.shape[0], stacked.shape[1], -1)


def gather_sources(value, chan_axes, seg_axis, companion):
    parts, sources, local_segs, freqs = value.shape
    count = lax.psum(1, chan_axes)
    segs = lax.psum(1, seg_axis)
    chunks = value.reshape(count, -1, freqs)
    rows = chunks.shape[1]
    if chan_axes == CHAN_AXES:
        pair = lax.psum(1, "c")
        rest = ("x", "zh", "y")
        upper = lax.axis_index("c") == 1
        flat = value.reshape(pair, -1, freqs)
        keep = jnp.where(upper, flat[1], flat[0])
        send = jnp.where(upper, flat[0], flat[1])
        half = keep + lax.ppermute(send, "c", [(0, 1), (1, 0)])
        part = half.reshape(count // pair, rows, freqs)
        mine = lax.all_to_all(part, rest, 0, 0).sum(axis=0, dtype=value.dtype)
        mine, companion = lax.optimization_barrier((mine, companion))
    else:
        mine = lax.all_to_all(chunks, chan_axes, 0, 0).sum(axis=0, dtype=value.dtype)
    if chan_axes == CHAN_AXES:
        spread = jnp.broadcast_to(mine[None], (count * segs // pair, rows, freqs))
        half_got = lax.all_to_all(spread, rest + (seg_axis,), 0, 0)
        sibling = lax.ppermute(half_got, "c", [(0, 1), (1, 0)])
        got = jnp.stack([half_got, sibling])
    else:
        spread = jnp.broadcast_to(mine[None], (count * segs, rows, freqs))
        got = lax.all_to_all(spread, chan_axes + (seg_axis,), 0, 0)
    split = local_segs // rows
    got = got.reshape(parts, sources, split, segs, rows, freqs).transpose(0, 3, 2, 4, 1, 5)
    return got.reshape(parts, segs * local_segs, sources, freqs), companion


def regroup_receivers(whitened, seg_axis):
    segs = lax.psum(1, seg_axis)
    me = lax.axis_index(seg_axis)
    parts, local_segs, ch_dev, freqs = whitened.shape
    groups = whitened.reshape(parts, local_segs, segs, ch_dev // segs, freqs)

    def group(index):
        return lax.dynamic_index_in_dim(groups, index, axis=2, keepdims=False)

    blocks = [group(me)]
    for shift in range(1, segs):
        pairs = [(i, (i + shift) % segs) for i in range(segs)]
        blocks.append(lax.ppermute(group((me + shift) % segs), seg_axis, pairs))
    rotated = jnp.concatenate(blocks[::-1], axis=1)
    doubled = jnp.concatenate([rotated, rotated], axis=1)
    start = ((segs - (me + 1) % segs) % segs) * local_segs
    return lax.dynamic_slice_in_dim(doubled, start, segs * local_segs, axis=1)


def make_shards(chan_axes):
    def shards(spectra, sources):
        whitened = whiten(spectra)
        regrouped = regroup_receivers(whitened, "seg")
        ch_dev = spectra.shape[2]
        freqs = spectra.shape[3]
        first_row = lax.axis_index(chan_axes) * ch_dev
        lag_table = lag_matrix(freqs, LAGS)
        local_row = sources.reshape(-1) - first_row
        onehot = (local_row[:, None] == jnp.arange(ch_dev, dtype=jnp.int32)[None, :]).astype(
            jnp.bfloat16
        )
        local_spec = jnp.einsum(
            "pc,xscf->xpsf", onehot, whitened, preferred_element_type=jnp.float32
        ).astype(jnp.bfloat16)
        source_spec, (regrouped, lag_table) = gather_sources(
            local_spec, chan_axes, "seg", (regrouped, lag_table)
        )
        swapped = lax.axis_index("c") == 1 if chan_axes == CHAN_AXES else False
        return correlate(source_spec, regrouped, lag_table, swapped)

    return shards


def solution(mesh):
    chan = mesh.shape["chan"]
    sizes = tuple(size for _, size in CHAN_FACTORS)
    if math.prod(sizes) == chan:
        devices = mesh.devices.reshape(sizes + (mesh.shape["seg"],))
        fine = Mesh(devices, CHAN_AXES + ("seg",))
        chan_axes = CHAN_AXES
    else:
        fine = mesh
        chan_axes = ("chan",)
    placed = (P(None, "seg", chan_axes, None), P())
    return jax.shard_map(
        make_shards(chan_axes),
        mesh=fine,
        in_specs=placed,
        out_specs=P(None, chan_axes + ("seg",), None),
        check_vma=False,
    )
```

```python
import math

import jax
import jax.numpy as jnp
from jax import lax
from jax.sharding import Mesh, PartitionSpec as P

LAGS = 256
CHAN_FACTORS = (("x", 4), ("zh", 2), ("y", 8), ("c", 2))
CHAN_AXES = tuple(name for name, _ in CHAN_FACTORS)


def whiten(spectra):
    values = spectra.astype(jnp.float32)
    power_mean = jnp.mean(values[0] * values[0] + values[1] * values[1], axis=-1)
    inv_scale = lax.rsqrt(power_mean + 1e-06)
    return (values * inv_scale[None, :, :, None]).astype(jnp.bfloat16)


def lag_matrix(freqs, half_lags):
    period = 2 * freqs
    rows = jnp.arange(freqs, dtype=jnp.int32)
    shifts = jnp.arange(2 * half_lags, dtype=jnp.int32) - half_lags
    phase = jnp.mod(rows[:, None] * shifts[None, :], period)
    angles = phase.astype(jnp.float32) * (2.0 * math.pi / period)
    return jnp.concatenate([jnp.cos(angles), -jnp.sin(angles)], axis=0)


def correlate(source_spec, receiver_spec, lag_table, swapped):
    segs = receiver_spec.shape[1]
    freqs = receiver_spec.shape[3]
    a = source_spec[0].astype(jnp.float32)[:, :, None, :]
    b = source_spec[1].astype(jnp.float32)[:, :, None, :]
    first = jnp.where(swapped, receiver_spec[1], receiver_spec[0])
    second = jnp.where(swapped, receiver_spec[0], receiver_spec[1])
    c = first.astype(jnp.float32)[:, None, :, :]
    d = second.astype(jnp.float32)[:, None, :, :]
    sign = jnp.where(swapped, -1.0, 1.0).astype(jnp.float32)
    real_part = jnp.sum(a * c + b * d, axis=0)
    imag_part = jnp.sum(a * d - b * c, axis=0) * sign
    stacked = jnp.concatenate([real_part, imag_part], axis=-1) * (1.0 / math.sqrt(segs))
    flat = stacked.reshape(-1, 2 * freqs)
    result = jnp.dot(
        flat, lag_table, precision=lax.Precision.HIGHEST, preferred_element_type=jnp.float32
    ) * (1.0 / math.sqrt(freqs))
    return result.reshape(stacked.shape[0], stacked.shape[1], -1)


def gather_sources(value, chan_axes, seg_axis, companion):
    parts, sources, local_segs, freqs = value.shape
    count = lax.psum(1, chan_axes)
    segs = lax.psum(1, seg_axis)
    chunks = value.reshape(count, -1, freqs)
    rows = chunks.shape[1]
    if chan_axes == CHAN_AXES:
        pair = lax.psum(1, "c")
        rest = ("x", "zh", "y")
        upper = lax.axis_index("c") == 1
        flat = value.reshape(pair, -1, freqs)
        keep = jnp.where(upper, flat[1], flat[0])
        send = jnp.where(upper, flat[0], flat[1])
        half = keep + lax.ppermute(send, "c", [(0, 1), (1, 0)])
        part = half.reshape(count // pair, rows, freqs)
        mine = lax.all_to_all(part, rest, 0, 0).sum(axis=0, dtype=value.dtype)
        mine, companion = lax.optimization_barrier((mine, companion))
    else:
        mine = lax.all_to_all(chunks, chan_axes, 0, 0).sum(axis=0, dtype=value.dtype)
    if chan_axes == CHAN_AXES:
        spread = jnp.broadcast_to(mine[None], (count * segs // pair, rows, freqs))
        half_got = lax.all_to_all(spread, rest + (seg_axis,), 0, 0)
        sibling = lax.ppermute(half_got, "c", [(0, 1), (1, 0)])
        got = jnp.stack([half_got, sibling])
    else:
        spread = jnp.broadcast_to(mine[None], (count * segs, rows, freqs))
        got = lax.all_to_all(spread, chan_axes + (seg_axis,), 0, 0)
    split = local_segs // rows
    got = got.reshape(parts, sources, split, segs, rows, freqs).transpose(0, 3, 2, 4, 1, 5)
    return got.reshape(parts, segs * local_segs, sources, freqs), companion


def regroup_receivers(whitened, seg_axis):
    segs = lax.psum(1, seg_axis)
    me = lax.axis_index(seg_axis)
    parts, local_segs, ch_dev, freqs = whitened.shape
    groups = whitened.reshape(parts, local_segs, segs, ch_dev // segs, freqs)

    def group(index):
        return lax.dynamic_index_in_dim(groups, index, axis=2, keepdims=False)

    blocks = [group(me)]
    for shift in range(1, segs):
        pairs = [(i, (i + shift) % segs) for i in range(segs)]
        blocks.append(lax.ppermute(group((me + shift) % segs), seg_axis, pairs))
    return jnp.concatenate(blocks[::-1], axis=1)


def rotate_segments(source_spec, seg_axis):
    segs = lax.psum(1, seg_axis)
    me = lax.axis_index(seg_axis)
    parts, all_segs, sources, freqs = source_spec.shape
    doubled = jnp.concatenate([source_spec, source_spec], axis=1)
    return lax.dynamic_slice_in_dim(doubled, ((me + 1) % segs) * (all_segs // segs), all_segs, axis=1)


def make_shards(chan_axes):
    def shards(spectra, sources):
        whitened = whiten(spectra)
        regrouped = regroup_receivers(whitened, "seg")
        ch_dev = spectra.shape[2]
        freqs = spectra.shape[3]
        first_row = lax.axis_index(chan_axes) * ch_dev
        lag_table = lag_matrix(freqs, LAGS)
        local_row = sources.reshape(-1) - first_row
        onehot = (local_row[:, None] == jnp.arange(ch_dev, dtype=jnp.int32)[None, :]).astype(
            jnp.bfloat16
        )
        local_spec = jnp.einsum(
            "pc,xscf->xpsf", onehot, whitened, preferred_element_type=jnp.float32
        ).astype(jnp.bfloat16)
        source_spec, (regrouped, lag_table) = gather_sources(
            local_spec, chan_axes, "seg", (regrouped, lag_table)
        )
        source_spec = rotate_segments(source_spec, "seg")
        swapped = lax.axis_index("c") == 1 if chan_axes == CHAN_AXES else False
        return correlate(source_spec, regrouped, lag_table, swapped)

    return shards


def solution(mesh):
    chan = mesh.shape["chan"]
    sizes = tuple(size for _, size in CHAN_FACTORS)
    if math.prod(sizes) == chan:
        devices = mesh.devices.reshape(sizes + (mesh.shape["seg"],))
        fine = Mesh(devices, CHAN_AXES + ("seg",))
        chan_axes = CHAN_AXES
    else:
        fine = mesh
        chan_axes = ("chan",)
    placed = (P(None, "seg", chan_axes, None), P())
    return jax.shard_map(
        make_shards(chan_axes),
        mesh=fine,
        in_specs=placed,
        out_specs=P(None, chan_axes + ("seg",), None),
        check_vma=False,
    )
```

```python
import math

import jax
import jax.numpy as jnp
from jax import lax
from jax.sharding import Mesh, PartitionSpec as P

LAGS = 256
CHAN_FACTORS = (("x", 4), ("zh", 2), ("y", 8), ("c", 2))
CHAN_AXES = tuple(name for name, _ in CHAN_FACTORS)


def whiten(spectra):
    values = spectra.astype(jnp.float32)
    power_mean = jnp.mean(values[0] * values[0] + values[1] * values[1], axis=-1)
    inv_scale = lax.rsqrt(power_mean + 1e-06)
    return (values * inv_scale[None, :, :, None]).astype(jnp.bfloat16)


def lag_matrix(freqs, half_lags):
    period = 2 * freqs
    rows = jnp.arange(freqs, dtype=jnp.int32)
    shifts = jnp.arange(2 * half_lags, dtype=jnp.int32) - half_lags
    phase = jnp.mod(rows[:, None] * shifts[None, :], period)
    angles = phase.astype(jnp.float32) * (2.0 * math.pi / period)
    return jnp.concatenate([jnp.cos(angles), -jnp.sin(angles)], axis=0)


def correlate(source_spec, receiver_spec, lag_table, swapped):
    segs = receiver_spec.shape[1]
    freqs = receiver_spec.shape[3]
    a = source_spec[0].astype(jnp.float32)[:, :, None, :]
    b = source_spec[1].astype(jnp.float32)[:, :, None, :]
    first = jnp.where(swapped, receiver_spec[1], receiver_spec[0])
    second = jnp.where(swapped, receiver_spec[0], receiver_spec[1])
    c = first.astype(jnp.float32)[:, None, :, :]
    d = second.astype(jnp.float32)[:, None, :, :]
    sign = jnp.where(swapped, -1.0, 1.0).astype(jnp.float32)
    real_part = jnp.sum(a * c + b * d, axis=0)
    imag_part = jnp.sum(a * d - b * c, axis=0) * sign
    stacked = jnp.concatenate([real_part, imag_part], axis=-1) * (1.0 / math.sqrt(segs))
    flat = stacked.reshape(-1, 2 * freqs)
    result = jnp.dot(
        flat, lag_table, precision=lax.Precision.HIGHEST, preferred_element_type=jnp.float32
    ) * (1.0 / math.sqrt(freqs))
    return result.reshape(stacked.shape[0], stacked.shape[1], -1)


def gather_sources(value, chan_axes, seg_axis, companion):
    parts, sources, local_segs, freqs = value.shape
    count = lax.psum(1, chan_axes)
    segs = lax.psum(1, seg_axis)
    chunks = value.reshape(count, -1, freqs)
    rows = chunks.shape[1]
    if chan_axes == CHAN_AXES:
        pair = lax.psum(1, "c")
        rest = ("x", "zh", "y")
        upper = lax.axis_index("c") == 1
        flat = value.reshape(pair, -1, freqs)
        keep = jnp.where(upper, flat[1], flat[0])
        send = jnp.where(upper, flat[0], flat[1])
        half = keep + lax.ppermute(send, "c", [(0, 1), (1, 0)])
        part = half.reshape(count // pair, rows, freqs)
        mine = lax.all_to_all(part, rest, 0, 0).sum(axis=0, dtype=value.dtype)
        mine, companion = lax.optimization_barrier((mine, companion))
    else:
        mine = lax.all_to_all(chunks, chan_axes, 0, 0).sum(axis=0, dtype=value.dtype)
    if chan_axes == CHAN_AXES:
        spread = jnp.broadcast_to(mine[None], (count * segs // pair, rows, freqs))
        half_got = lax.all_to_all(spread, rest + (seg_axis,), 0, 0)
        sibling = lax.ppermute(half_got, "c", [(0, 1), (1, 0)])
        got = jnp.stack([half_got, sibling])
    else:
        spread = jnp.broadcast_to(mine[None], (count * segs, rows, freqs))
        got = lax.all_to_all(spread, chan_axes + (seg_axis,), 0, 0)
    split = local_segs // rows
    got = got.reshape(parts, sources, split, segs, rows, freqs).transpose(0, 3, 2, 4, 1, 5)
    return got.reshape(parts, segs * local_segs, sources, freqs), companion


def regroup_receivers(whitened, seg_axis):
    segs = lax.psum(1, seg_axis)
    me = lax.axis_index(seg_axis)
    parts, local_segs, ch_dev, freqs = whitened.shape
    groups = whitened.reshape(parts, local_segs, segs, ch_dev // segs, freqs)

    def group(index):
        return lax.dynamic_index_in_dim(groups, index, axis=2, keepdims=False)

    blocks = [group(me)]
    for shift in range(1, segs):
        pairs = [(i, (i + shift) % segs) for i in range(segs)]
        blocks.append(lax.ppermute(group((me + shift) % segs), seg_axis, pairs))
    return jnp.concatenate(blocks[::-1], axis=1)


def unrotate_segments(spec, seg_axis):
    segs = lax.psum(1, seg_axis)
    me = lax.axis_index(seg_axis)
    all_segs = spec.shape[1]
    doubled = jnp.concatenate([spec, spec], axis=1)
    start = ((segs - (me + 1) % segs) % segs) * (all_segs // segs)
    return lax.dynamic_slice_in_dim(doubled, start, all_segs, axis=1)


def make_shards(chan_axes):
    def shards(spectra, sources):
        whitened = whiten(spectra)
        regrouped = regroup_receivers(whitened, "seg")
        ch_dev = spectra.shape[2]
        freqs = spectra.shape[3]
        first_row = lax.axis_index(chan_axes) * ch_dev
        lag_table = lag_matrix(freqs, LAGS)
        local_row = sources.reshape(-1) - first_row
        onehot = (local_row[:, None] == jnp.arange(ch_dev, dtype=jnp.int32)[None, :]).astype(
            jnp.bfloat16
        )
        local_spec = jnp.einsum(
            "pc,xscf->xpsf", onehot, whitened, preferred_element_type=jnp.float32
        ).astype(jnp.bfloat16)
        source_spec, (regrouped, lag_table) = gather_sources(
            local_spec, chan_axes, "seg", (regrouped, lag_table)
        )
        regrouped = unrotate_segments(regrouped, "seg")
        swapped = lax.axis_index("c") == 1 if chan_axes == CHAN_AXES else False
        return correlate(source_spec, regrouped, lag_table, swapped)

    return shards


def solution(mesh):
    chan = mesh.shape["chan"]
    sizes = tuple(size for _, size in CHAN_FACTORS)
    if math.prod(sizes) == chan:
        devices = mesh.devices.reshape(sizes + (mesh.shape["seg"],))
        fine = Mesh(devices, CHAN_AXES + ("seg",))
        chan_axes = CHAN_AXES
    else:
        fine = mesh
        chan_axes = ("chan",)
    placed = (P(None, "seg", chan_axes, None), P())
    return jax.shard_map(
        make_shards(chan_axes),
        mesh=fine,
        in_specs=placed,
        out_specs=P(None, chan_axes + ("seg",), None),
        check_vma=False,
    )
```

```python
import math

import jax
import jax.numpy as jnp
from jax import lax
from jax.sharding import Mesh, PartitionSpec as P

LAGS = 256
CHAN_FACTORS = (("x", 4), ("zh", 2), ("y", 8), ("c", 2))
CHAN_AXES = tuple(name for name, _ in CHAN_FACTORS)


def whiten(spectra):
    values = spectra.astype(jnp.float32)
    power_mean = jnp.mean(values[0] * values[0] + values[1] * values[1], axis=-1)
    inv_scale = lax.rsqrt(power_mean + 1e-06)
    return (values * inv_scale[None, :, :, None]).astype(jnp.bfloat16)


def lag_matrix(freqs, half_lags):
    period = 2 * freqs
    rows = jnp.arange(freqs, dtype=jnp.int32)
    shifts = jnp.arange(2 * half_lags, dtype=jnp.int32) - half_lags
    phase = jnp.mod(rows[:, None] * shifts[None, :], period)
    angles = phase.astype(jnp.float32) * (2.0 * math.pi / period)
    return jnp.concatenate([jnp.cos(angles), -jnp.sin(angles)], axis=0)


def correlate(source_spec, receiver_spec, lag_table, swapped):
    segs = receiver_spec.shape[1]
    freqs = receiver_spec.shape[3]
    a = source_spec[0].astype(jnp.float32)[:, :, None, :]
    b = source_spec[1].astype(jnp.float32)[:, :, None, :]
    first = jnp.where(swapped, receiver_spec[1], receiver_spec[0])
    second = jnp.where(swapped, receiver_spec[0], receiver_spec[1])
    c = first.astype(jnp.float32)[None]
    d = second.astype(jnp.float32)[None]
    sign = jnp.where(swapped, -1.0, 1.0).astype(jnp.float32)
    real_part = jnp.sum(a * c + b * d, axis=1)
    imag_part = jnp.sum(a * d - b * c, axis=1) * sign
    stacked = jnp.concatenate([real_part, imag_part], axis=-1) * (1.0 / math.sqrt(segs))
    flat = stacked.reshape(-1, 2 * freqs)
    result = jnp.dot(
        flat, lag_table, precision=lax.Precision.HIGHEST, preferred_element_type=jnp.float32
    ) * (1.0 / math.sqrt(freqs))
    return result.reshape(stacked.shape[0], stacked.shape[1], -1)


def gather_sources(value, chan_axes, seg_axis, companion):
    parts, sources, local_segs, freqs = value.shape
    count = lax.psum(1, chan_axes)
    segs = lax.psum(1, seg_axis)
    chunks = value.reshape(count, -1, freqs)
    rows = chunks.shape[1]
    if chan_axes == CHAN_AXES:
        pair = lax.psum(1, "c")
        rest = ("x", "zh", "y")
        upper = lax.axis_index("c") == 1
        flat = value.reshape(pair, -1, freqs)
        keep = jnp.where(upper, flat[1], flat[0])
        send = jnp.where(upper, flat[0], flat[1])
        half = keep + lax.ppermute(send, "c", [(0, 1), (1, 0)])
        part = half.reshape(count // pair, rows, freqs)
        mine = lax.all_to_all(part, rest, 0, 0).sum(axis=0, dtype=value.dtype)
        mine, companion = lax.optimization_barrier((mine, companion))
    else:
        mine = lax.all_to_all(chunks, chan_axes, 0, 0).sum(axis=0, dtype=value.dtype)
    if chan_axes == CHAN_AXES:
        spread = jnp.broadcast_to(mine[None], (count * segs // pair, rows, freqs))
        half_got = lax.all_to_all(spread, rest + (seg_axis,), 0, 0)
        sibling = lax.ppermute(half_got, "c", [(0, 1), (1, 0)])
        got = jnp.stack([half_got, sibling])
    else:
        spread = jnp.broadcast_to(mine[None], (count * segs, rows, freqs))
        got = lax.all_to_all(spread, chan_axes + (seg_axis,), 0, 0)
    split = local_segs // rows
    return got.reshape(parts, sources, segs * local_segs, freqs), companion


def slot_order(spec, segs, rows):
    parts, all_segs, receivers, freqs = spec.shape
    split = all_segs // (segs * rows)
    spec = spec.reshape(parts, segs, split, rows, receivers, freqs).transpose(0, 2, 1, 3, 4, 5)
    return spec.reshape(parts, all_segs, receivers, freqs)


def regroup_receivers(whitened, seg_axis):
    segs = lax.psum(1, seg_axis)
    me = lax.axis_index(seg_axis)
    parts, local_segs, ch_dev, freqs = whitened.shape
    groups = whitened.reshape(parts, local_segs, segs, ch_dev // segs, freqs)

    def group(index):
        return lax.dynamic_index_in_dim(groups, index, axis=2, keepdims=False)

    blocks = [group(me)]
    for shift in range(1, segs):
        pairs = [(i, (i + shift) % segs) for i in range(segs)]
        blocks.append(lax.ppermute(group((me + shift) % segs), seg_axis, pairs))
    return jnp.concatenate(blocks[::-1], axis=1)


def unrotate_segments(spec, seg_axis):
    segs = lax.psum(1, seg_axis)
    me = lax.axis_index(seg_axis)
    all_segs = spec.shape[1]
    doubled = jnp.concatenate([spec, spec], axis=1)
    start = ((segs - (me + 1) % segs) % segs) * (all_segs // segs)
    return lax.dynamic_slice_in_dim(doubled, start, all_segs, axis=1)


def make_shards(chan_axes):
    def shards(spectra, sources):
        whitened = whiten(spectra)
        regrouped = regroup_receivers(whitened, "seg")
        ch_dev = spectra.shape[2]
        freqs = spectra.shape[3]
        first_row = lax.axis_index(chan_axes) * ch_dev
        lag_table = lag_matrix(freqs, LAGS)
        local_row = sources.reshape(-1) - first_row
        onehot = (local_row[:, None] == jnp.arange(ch_dev, dtype=jnp.int32)[None, :]).astype(
            jnp.bfloat16
        )
        local_spec = jnp.einsum(
            "pc,xscf->xpsf", onehot, whitened, preferred_element_type=jnp.float32
        ).astype(jnp.bfloat16)
        source_spec, (regrouped, lag_table) = gather_sources(
            local_spec, chan_axes, "seg", (regrouped, lag_table)
        )
        regrouped = unrotate_segments(regrouped, "seg")
        rows = local_spec.size // (lax.psum(1, chan_axes) * freqs)
        regrouped = slot_order(regrouped, lax.psum(1, "seg"), rows)
        swapped = lax.axis_index("c") == 1 if chan_axes == CHAN_AXES else False
        return correlate(source_spec, regrouped, lag_table, swapped)

    return shards


def solution(mesh):
    chan = mesh.shape["chan"]
    sizes = tuple(size for _, size in CHAN_FACTORS)
    if math.prod(sizes) == chan:
        devices = mesh.devices.reshape(sizes + (mesh.shape["seg"],))
        fine = Mesh(devices, CHAN_AXES + ("seg",))
        chan_axes = CHAN_AXES
    else:
        fine = mesh
        chan_axes = ("chan",)
    placed = (P(None, "seg", chan_axes, None), P())
    return jax.shard_map(
        make_shards(chan_axes),
        mesh=fine,
        in_specs=placed,
        out_specs=P(None, chan_axes + ("seg",), None),
        check_vma=False,
    )
```

```python
import math

import jax
import jax.numpy as jnp
from jax import lax
from jax.sharding import Mesh, PartitionSpec as P

LAGS = 256
CHAN_FACTORS = (("x", 4), ("zh", 2), ("y", 8), ("c", 2))
CHAN_AXES = tuple(name for name, _ in CHAN_FACTORS)


def whiten(spectra):
    values = spectra.astype(jnp.float32)
    power_mean = jnp.mean(values[0] * values[0] + values[1] * values[1], axis=-1)
    inv_scale = lax.rsqrt(power_mean + 1e-06)
    return (values * inv_scale[None, :, :, None]).astype(jnp.bfloat16)


def lag_matrix(freqs, half_lags):
    period = 2 * freqs
    rows = jnp.arange(freqs, dtype=jnp.int32)
    shifts = jnp.arange(2 * half_lags, dtype=jnp.int32) - half_lags
    phase = jnp.mod(rows[:, None] * shifts[None, :], period)
    angles = phase.astype(jnp.float32) * (2.0 * math.pi / period)
    return jnp.concatenate([jnp.cos(angles), -jnp.sin(angles)], axis=0)


def correlate(source_spec, receiver_spec, lag_table, swapped):
    segs = receiver_spec.shape[1]
    freqs = receiver_spec.shape[3]
    a = source_spec[0].astype(jnp.float32)[:, :, None, :]
    b = source_spec[1].astype(jnp.float32)[:, :, None, :]
    first = jnp.where(swapped, receiver_spec[1], receiver_spec[0])
    second = jnp.where(swapped, receiver_spec[0], receiver_spec[1])
    c = first.astype(jnp.float32)[:, None, :, :]
    d = second.astype(jnp.float32)[:, None, :, :]
    sign = jnp.where(swapped, -1.0, 1.0).astype(jnp.float32)
    real_part = jnp.sum(a * c, axis=0) + jnp.sum(b * d, axis=0)
    imag_part = (jnp.sum(a * d, axis=0) - jnp.sum(b * c, axis=0)) * sign
    stacked = jnp.concatenate([real_part, imag_part], axis=-1) * (1.0 / math.sqrt(segs))
    flat = stacked.reshape(-1, 2 * freqs)
    result = jnp.dot(
        flat, lag_table, precision=lax.Precision.HIGHEST, preferred_element_type=jnp.float32
    ) * (1.0 / math.sqrt(freqs))
    return result.reshape(stacked.shape[0], stacked.shape[1], -1)


def gather_sources(value, chan_axes, seg_axis, companion):
    parts, sources, local_segs, freqs = value.shape
    count = lax.psum(1, chan_axes)
    segs = lax.psum(1, seg_axis)
    chunks = value.reshape(count, -1, freqs)
    rows = chunks.shape[1]
    if chan_axes == CHAN_AXES:
        pair = lax.psum(1, "c")
        rest = ("x", "zh", "y")
        upper = lax.axis_index("c") == 1
        flat = value.reshape(pair, -1, freqs)
        keep = jnp.where(upper, flat[1], flat[0])
        send = jnp.where(upper, flat[0], flat[1])
        half = keep + lax.ppermute(send, "c", [(0, 1), (1, 0)])
        part = half.reshape(count // pair, rows, freqs)
        mine = lax.all_to_all(part, rest, 0, 0).sum(axis=0, dtype=value.dtype)
        mine, companion = lax.optimization_barrier((mine, companion))
    else:
        mine = lax.all_to_all(chunks, chan_axes, 0, 0).sum(axis=0, dtype=value.dtype)
    if chan_axes == CHAN_AXES:
        spread = jnp.broadcast_to(mine[None], (count * segs // pair, rows, freqs))
        half_got = lax.all_to_all(spread, rest + (seg_axis,), 0, 0)
        sibling = lax.ppermute(half_got, "c", [(0, 1), (1, 0)])
        halves = [half_got, sibling]
    else:
        spread = jnp.broadcast_to(mine[None], (count * segs, rows, freqs))
        got = lax.all_to_all(spread, chan_axes + (seg_axis,), 0, 0)
        halves = list(got.reshape(parts, -1, rows, freqs))
    split = local_segs // rows
    halves = [
        half.reshape(sources, split, segs, rows, freqs)
        .transpose(2, 1, 3, 0, 4)
        .reshape(segs * local_segs, sources, freqs)
        for half in halves
    ]
    return halves, companion


def regroup_receivers(whitened, seg_axis):
    segs = lax.psum(1, seg_axis)
    me = lax.axis_index(seg_axis)
    parts, local_segs, ch_dev, freqs = whitened.shape
    groups = whitened.reshape(parts, local_segs, segs, ch_dev // segs, freqs)

    def group(index):
        return lax.dynamic_index_in_dim(groups, index, axis=2, keepdims=False)

    blocks = [group(me)]
    for shift in range(1, segs):
        pairs = [(i, (i + shift) % segs) for i in range(segs)]
        blocks.append(lax.ppermute(group((me + shift) % segs), seg_axis, pairs))
    return jnp.concatenate(blocks[::-1], axis=1)


def unrotate_segments(spec, seg_axis):
    segs = lax.psum(1, seg_axis)
    me = lax.axis_index(seg_axis)
    all_segs = spec.shape[1]
    doubled = jnp.concatenate([spec, spec], axis=1)
    start = ((segs - (me + 1) % segs) % segs) * (all_segs // segs)
    return lax.dynamic_slice_in_dim(doubled, start, all_segs, axis=1)


def make_shards(chan_axes):
    def shards(spectra, sources):
        whitened = whiten(spectra)
        regrouped = regroup_receivers(whitened, "seg")
        ch_dev = spectra.shape[2]
        freqs = spectra.shape[3]
        first_row = lax.axis_index(chan_axes) * ch_dev
        lag_table = lag_matrix(freqs, LAGS)
        local_row = sources.reshape(-1) - first_row
        onehot = (local_row[:, None] == jnp.arange(ch_dev, dtype=jnp.int32)[None, :]).astype(
            jnp.bfloat16
        )
        local_spec = jnp.einsum(
            "pc,xscf->xpsf", onehot, whitened, preferred_element_type=jnp.float32
        ).astype(jnp.bfloat16)
        source_spec, (regrouped, lag_table) = gather_sources(
            local_spec, chan_axes, "seg", (regrouped, lag_table)
        )
        regrouped = unrotate_segments(regrouped, "seg")
        swapped = lax.axis_index("c") == 1 if chan_axes == CHAN_AXES else False
        return correlate(source_spec, regrouped, lag_table, swapped)

    return shards


def solution(mesh):
    chan = mesh.shape["chan"]
    sizes = tuple(size for _, size in CHAN_FACTORS)
    if math.prod(sizes) == chan:
        devices = mesh.devices.reshape(sizes + (mesh.shape["seg"],))
        fine = Mesh(devices, CHAN_AXES + ("seg",))
        chan_axes = CHAN_AXES
    else:
        fine = mesh
        chan_axes = ("chan",)
    placed = (P(None, "seg", chan_axes, None), P())
    return jax.shard_map(
        make_shards(chan_axes),
        mesh=fine,
        in_specs=placed,
        out_specs=P(None, chan_axes + ("seg",), None),
        check_vma=False,
    )
```

```python
import math

import jax
import jax.numpy as jnp
from jax import lax
from jax.sharding import Mesh, PartitionSpec as P

LAGS = 256
CHAN_FACTORS = (("x", 4), ("zh", 2), ("y", 8), ("c", 2))
CHAN_AXES = tuple(name for name, _ in CHAN_FACTORS)


def whiten(spectra):
    values = spectra.astype(jnp.float32)
    power_mean = jnp.mean(values[0] * values[0] + values[1] * values[1], axis=-1)
    inv_scale = lax.rsqrt(power_mean + 1e-06)
    return (values * inv_scale[None, :, :, None]).astype(jnp.bfloat16)


def lag_matrix(freqs, half_lags):
    period = 2 * freqs
    rows = jnp.arange(freqs, dtype=jnp.int32)
    shifts = jnp.arange(2 * half_lags, dtype=jnp.int32) - half_lags
    phase = jnp.mod(rows[:, None] * shifts[None, :], period)
    angles = phase.astype(jnp.float32) * (2.0 * math.pi / period)
    return jnp.concatenate([jnp.cos(angles), -jnp.sin(angles)], axis=0)


def correlate(source_spec, receiver_spec, lag_table, swapped):
    segs = receiver_spec.shape[1]
    freqs = receiver_spec.shape[3]
    a = source_spec[0].astype(jnp.float32)[:, :, None, :]
    b = source_spec[1].astype(jnp.float32)[:, :, None, :]
    first = jnp.where(swapped, receiver_spec[1], receiver_spec[0])
    second = jnp.where(swapped, receiver_spec[0], receiver_spec[1])
    c = first.astype(jnp.float32)[:, None, :, :]
    d = second.astype(jnp.float32)[:, None, :, :]
    sign = jnp.where(swapped, -1.0, 1.0).astype(jnp.float32)
    real_part = jnp.sum(a * c + b * d, axis=0)
    imag_part = jnp.sum(a * d - b * c, axis=0) * sign
    stacked = jnp.concatenate([real_part, imag_part], axis=-1) * (1.0 / math.sqrt(segs))
    flat = stacked.reshape(-1, 2 * freqs)
    result = jnp.dot(
        flat, lag_table, precision=lax.Precision.HIGHEST, preferred_element_type=jnp.float32
    ) * (1.0 / math.sqrt(freqs))
    return result.reshape(stacked.shape[0], stacked.shape[1], -1)


def gather_sources(value, chan_axes, seg_axis, companion):
    parts, sources, local_segs, freqs = value.shape
    count = lax.psum(1, chan_axes)
    segs = lax.psum(1, seg_axis)
    chunks = value.reshape(count, -1, freqs)
    rows = chunks.shape[1]
    if chan_axes == CHAN_AXES:
        pair = lax.psum(1, "c")
        rest = ("x", "zh", "y")
        upper = lax.axis_index("c") == 1
        mine = lax.all_to_all(chunks, ("c",) + rest, 0, 0).sum(axis=0, dtype=value.dtype)
        mine, companion = lax.optimization_barrier((mine, companion))
    else:
        mine = lax.all_to_all(chunks, chan_axes, 0, 0).sum(axis=0, dtype=value.dtype)
    if chan_axes == CHAN_AXES:
        spread = jnp.broadcast_to(mine[None], (count * segs // pair, rows, freqs))
        half_got = lax.all_to_all(spread, rest + (seg_axis,), 0, 0)
        sibling = lax.ppermute(half_got, "c", [(0, 1), (1, 0)])
        got = jnp.stack([half_got, sibling])
    else:
        spread = jnp.broadcast_to(mine[None], (count * segs, rows, freqs))
        got = lax.all_to_all(spread, chan_axes + (seg_axis,), 0, 0)
    split = local_segs // rows
    got = got.reshape(parts, sources, split, segs, rows, freqs).transpose(0, 3, 2, 4, 1, 5)
    return got.reshape(parts, segs * local_segs, sources, freqs), companion


def regroup_receivers(whitened, seg_axis):
    segs = lax.psum(1, seg_axis)
    me = lax.axis_index(seg_axis)
    parts, local_segs, ch_dev, freqs = whitened.shape
    groups = whitened.reshape(parts, local_segs, segs, ch_dev // segs, freqs)

    def group(index):
        return lax.dynamic_index_in_dim(groups, index, axis=2, keepdims=False)

    blocks = [group(me)]
    for shift in range(1, segs):
        pairs = [(i, (i + shift) % segs) for i in range(segs)]
        blocks.append(lax.ppermute(group((me + shift) % segs), seg_axis, pairs))
    return jnp.concatenate(blocks[::-1], axis=1)


def unrotate_segments(spec, seg_axis):
    segs = lax.psum(1, seg_axis)
    me = lax.axis_index(seg_axis)
    all_segs = spec.shape[1]
    doubled = jnp.concatenate([spec, spec], axis=1)
    start = ((segs - (me + 1) % segs) % segs) * (all_segs // segs)
    return lax.dynamic_slice_in_dim(doubled, start, all_segs, axis=1)


def make_shards(chan_axes):
    def shards(spectra, sources):
        whitened = whiten(spectra)
        regrouped = regroup_receivers(whitened, "seg")
        ch_dev = spectra.shape[2]
        freqs = spectra.shape[3]
        first_row = lax.axis_index(chan_axes) * ch_dev
        lag_table = lag_matrix(freqs, LAGS)
        local_row = sources.reshape(-1) - first_row
        onehot = (local_row[:, None] == jnp.arange(ch_dev, dtype=jnp.int32)[None, :]).astype(
            jnp.bfloat16
        )
        local_spec = jnp.einsum(
            "pc,xscf->xpsf", onehot, whitened, preferred_element_type=jnp.float32
        ).astype(jnp.bfloat16)
        source_spec, (regrouped, lag_table) = gather_sources(
            local_spec, chan_axes, "seg", (regrouped, lag_table)
        )
        regrouped = unrotate_segments(regrouped, "seg")
        swapped = lax.axis_index("c") == 1 if chan_axes == CHAN_AXES else False
        return correlate(source_spec, regrouped, lag_table, swapped)

    return shards


def solution(mesh):
    chan = mesh.shape["chan"]
    sizes = tuple(size for _, size in CHAN_FACTORS)
    if math.prod(sizes) == chan:
        devices = mesh.devices.reshape(sizes + (mesh.shape["seg"],))
        fine = Mesh(devices, CHAN_AXES + ("seg",))
        chan_axes = CHAN_AXES
    else:
        fine = mesh
        chan_axes = ("chan",)
    placed = (P(None, "seg", chan_axes, None), P())
    return jax.shard_map(
        make_shards(chan_axes),
        mesh=fine,
        in_specs=placed,
        out_specs=P(None, chan_axes + ("seg",), None),
        check_vma=False,
    )
```
